256 devices in a mesh: req: 8 (over z), exp: 32 (over y, x, core).
Axes of the slice: x: 4, y: 4, z: 8, core: 2. Of those that a mesh axis runs over, the one named last changes fastest.
Arguments:
- residual: bfloat16 [32768, 1536], P(('req', 'exp')), may hold values from -2 to 2
- queries: bfloat16 [32768, 1536], P(('req', 'exp')), may hold values from -8 to 8
- suffix_key_values: bfloat16 [2, 32768, 256], P(None, ('req', 'exp')), may hold values from -8 to 8
- prefix_key_values: bfloat16 [2, 4096, 256], P(None, ('req', 'exp')), may hold values from -6 to 6
- request_ids: int32 [256, 128], P(('req', 'exp')), may hold values from 0 to 3, never falling along the last dimension, each value on 1 to 64 neighbouring positions
- out_weight: bfloat16 [1536, 1536], P('req'), may hold values from -0.15625 to 0.15625
- norm_gain: float32 [1536], replicated, may hold values from 0.5 to 1.5
- expert_routes: int32 [32768, 4], P(('req', 'exp')), may hold values from 0 to 31, all different within a row; in each aligned block of 128 rows (0 to 127, 128 to 255, ...) at most 24 rows name the same one
- route_gates: float32 [32768, 4], P(('req', 'exp')), may hold values from 0.1 to 0.6
- gate_experts: bfloat16 [32, 1536, 768], P('exp'), may hold values from -0.15625 to 0.15625
- up_experts: bfloat16 [32, 1536, 768], P('exp'), may hold values from -0.15625 to 0.15625
- down_experts: bfloat16 [32, 768, 1536], P('exp'), may hold values from -0.21875 to 0.21875
Outputs:
- layer_out: bfloat16 [32768, 1536], P(('req', 'exp'))
The draws below stay inside these ranges and needn't reach their ends.
Inputs may be any that keep to these rules, and one draw needn't show every extreme that they name: `expert_routes`: in the rows of one device no expert is named by more than 24 routes, a bound that some block reaches of them; a row names 4 different experts. `request_ids`: along a row the numbers never fall; each number marks one request of 1 to 64 tokens, and one request in the row has exactly 64.
All inputs are finite; a program needn't handle non-finite values.
Results may differ from the reference program's by a relative error of at most 0.013.
Values may be sent and summed in bfloat16 or wider, within the bound.
No kernel may reach another device: no remote copies, remote signals or barrier semaphores. Data moves between devices by JAX's collectives and lax.ppermute only.
A program may use at most 64 MiB of HBM per device.

```python
import math
import jax
import jax.numpy as jnp
import numpy as np
from jax import lax

D = 1536
QUERY_HEADS = 12
KEY_VALUE_HEADS = 2
HEAD_SIZE = 128
F = 768
TOP = 4
PREFIX_TOKENS = 4096
REQS = 4
DEVICE_TOKENS = 128
EXPERTS = 32
CAP = 24
SUFFIX_TOKENS = 32768
N_REQ = 8
N_EXP = 32


def draw_queries(key, part):
    start_offset = jnp.clip(jax.random.normal(jax.random.fold_in(key, 3), (SUFFIX_TOKENS, D), jnp.float32) * 2.0, -8.0, 8.0)
    return start_offset.astype(jnp.bfloat16)


def draw_prefix_key_values(key, part):
    start_offset = jnp.clip(jax.random.normal(jax.random.fold_in(key, 13), (2, PREFIX_TOKENS, KEY_VALUE_HEADS * HEAD_SIZE), jnp.float32), -6.0, 6.0)
    return start_offset.astype(jnp.bfloat16)


def steps_of(key, dims, split, low, largest):
    level = 1.0
    for dim, parts in split:
        steps = jax.random.uniform(jax.random.fold_in(jax.random.fold_in(key, 6), dim), (parts,), jnp.float32, low / len(split), largest / len(split))
        level = level * jnp.repeat(jnp.exp(steps), dims[dim] // parts).reshape((-1,) + (1,) * (len(dims) - 1 - dim))
    return level


def split_up(number_of, total, limit, skew):
    weights = [(1 << 20) // math.isqrt(standing ** skew) + 1 for standing in range(2, number_of + 1)]
    surplus, given = total - limit - (number_of - 1), [1] * (number_of - 1)
    while surplus > 0:
        movable = [i for i in range(number_of - 1) if given[i] < limit]
        mass, left = sum([weights[i] for i in movable]), surplus
        for i in movable:
            more = min(limit - given[i], max(1, left * weights[i] // mass), surplus)
            given[i] = given[i] + more
            surplus = surplus - more
    return np.array([limit] + given)


def uneven(own_key, amount, total, most, skew):
    if amount == 2:
        one = jax.random.randint(own_key, (), max(1, total - most), min(most, total - 1) + 1)
        return jnp.stack([one, total - one])
    lengths = jnp.asarray(split_up(amount, total, most, skew), jnp.int32)
    couples = (amount - 1) // 2
    giver, sink = lengths[1:1 + 2 * couples:2], lengths[2:2 + 2 * couples:2]
    margin = jnp.minimum(giver - 1, most - sink)
    moved = jax.random.randint(jax.random.fold_in(own_key, 1), (couples,), 0, 1 << 20) % (margin + 1)
    lengths = lengths.at[1:1 + 2 * couples:2].set(giver - moved).at[2:2 + 2 * couples:2].set(sink + moved)
    return lengths[jax.random.permutation(jax.random.fold_in(own_key, 2), amount)]


def assign_block(stream_key, own, number, rows, number_of, top, reach, lean):
    sequence = jax.random.permutation(stream_key, number_of)
    heavy_load, ordinary = portions_of(number_of, rows * top, reach, lean, True), portions_of(number_of, rows * top, reach, lean, False)
    places = jnp.arange(number_of)

    def named(sizes, rotation):
        used = int((sizes > 0).sum())
        fixed = max(1, used // 4)
        shifted = fixed + (places - fixed + rotation * (used - fixed)) % max(1, number_of - fixed)
        return jnp.zeros((number_of,), jnp.int32).at[sequence[jnp.where(places < fixed, places, shifted)]].set(jnp.asarray(sizes, jnp.int32))

    sizes = jnp.where(number % 4 == 0, named(heavy_load, number // 4), named(ordinary, number - number // 4 - 1))
    mixed = jax.random.permutation(jax.random.fold_in(own, 3), number_of)
    source_of, receiver = mixed[0:number_of // 2 * 2:2], mixed[1:number_of // 2 * 2:2]
    margin = jnp.minimum(sizes[source_of] - 1, reach - sizes[receiver]) // 2
    margin = jnp.where((source_of == sequence[0]) | (receiver == sequence[0]) | (sizes[receiver] == 0), 0, jnp.maximum(margin, 0))
    shifted = jax.random.randint(jax.random.fold_in(own, 4), (number_of // 2,), 0, 1 << 20) % (margin + 1)
    sizes = sizes.at[source_of].add(-shifted).at[receiver].add(shifted)
    items = jnp.searchsorted(jnp.cumsum(sizes), jnp.arange(rows * top), side="right").astype(jnp.int32)
    listing = items.reshape(top, rows).T
    listing = listing[jax.random.permutation(jax.random.fold_in(own, 1), rows)]
    rotation = jax.random.randint(jax.random.fold_in(own, 2), (rows, 1), 0, top)
    return jnp.take_along_axis(listing, (jnp.arange(top)[None, :] + rotation) % top, axis=1)


def portions_of(number_of, total, bound, skew, full):
    portions = [(1 << 20) // math.isqrt(standing ** skew) + 1 for standing in range(1, number_of + 1)]
    largest = bound if full else min(bound, max(-(-total // number_of), total * portions[0] // sum(portions)))
    least = 1 if total - largest >= number_of - 1 else 0
    holding, surplus = [largest] + [least] * (number_of - 1), total - largest - least * (number_of - 1)
    while surplus > 0:
        movable = [i for i in range(1, number_of) if holding[i] < largest] or [i for i in range(1, number_of) if holding[i] < bound]
        whole, remaining = sum([portions[i] for i in movable]), surplus
        for i in movable:
            more = min(bound - holding[i], max(1, remaining * portions[i] // whole), surplus)
            holding[i] = holding[i] + more
            surplus = surplus - more
    return np.array(holding)


def scatter_about(rng, dims, width, most, split=(), held_as=jnp.bfloat16):
    gain = steps_of(rng, dims, split, -0.22, 0.18) if split else 1.0
    array = jax.random.normal(rng, dims, jnp.float32) * width * gain
    return jnp.minimum(jnp.maximum(array, -most), most).astype(held_as)


def setup_inputs(seed: int = 0) -> dict:
    streams_of = jax.random.split(jax.random.key(seed), 13)
    residual = scatter_about(streams_of[0], (SUFFIX_TOKENS, D), 0.3, 2.0, ((0, 256),))
    queries = draw_queries(jax.random.fold_in(streams_of[12], 71), 0)
    suffix_key_values = scatter_about(streams_of[2], (2, SUFFIX_TOKENS, KEY_VALUE_HEADS * HEAD_SIZE), 1.3, 8.0, ((1, 256),))
    prefix_key_values = draw_prefix_key_values(jax.random.fold_in(streams_of[12], 71), 0)
    request_ids = jax.vmap(lambda own: jnp.searchsorted(jnp.cumsum(uneven(own, REQS, DEVICE_TOKENS, DEVICE_TOKENS // 2, 2)), jnp.arange(DEVICE_TOKENS), side="right"))(jax.random.split(streams_of[4], (N_REQ * N_EXP))).reshape((N_REQ * N_EXP, DEVICE_TOKENS)).astype(jnp.int32)
    out_weight = scatter_about(streams_of[5], (D, D), D ** -0.5, 0.15625, ((0, 8),))
    norm_gain = jnp.clip(1.0 + 0.1 * jax.random.normal(streams_of[6], (D,), jnp.float32), 0.5, 1.5)
    expert_routes_keys = jax.random.split(jax.random.fold_in(streams_of[7], 1), SUFFIX_TOKENS // DEVICE_TOKENS)
    expert_routes_turns = jax.random.permutation(jax.random.fold_in(streams_of[7], 3), SUFFIX_TOKENS // DEVICE_TOKENS)
    expert_routes = jax.vmap(lambda own, number: assign_block(jax.random.fold_in(streams_of[7], 2), own, number, DEVICE_TOKENS, EXPERTS, TOP, CAP, 2))(expert_routes_keys, expert_routes_turns).reshape((SUFFIX_TOKENS, TOP))
    route_gates = jnp.clip(0.1 + 0.5 * jax.random.uniform(streams_of[8], (SUFFIX_TOKENS, TOP), jnp.float32) ** steps_of(streams_of[8], (SUFFIX_TOKENS, TOP), ((0, 256),), -0.2, 0.2), 0.1, 0.6)
    gate_experts = scatter_about(streams_of[9], (EXPERTS, D, F), D ** -0.5, 0.15625, ((0, 32),))
    up_experts = scatter_about(streams_of[10], (EXPERTS, D, F), D ** -0.5, 0.15625, ((0, 32),))
    down_experts = scatter_about(streams_of[11], (EXPERTS, F, D), F ** -0.5, 0.21875, ((0, 32),))
    return {"residual": residual, "queries": queries, "suffix_key_values": suffix_key_values, "prefix_key_values": prefix_key_values, "request_ids": request_ids, "out_weight": out_weight, "norm_gain": norm_gain, "expert_routes": expert_routes, "route_gates": route_gates, "gate_experts": gate_experts, "up_experts": up_experts, "down_experts": down_experts}


EPSILON = 1e-06
MASKED_SCORE = -1e+30

def attend_block(query_block_rows, suffix_of_block, block_ids, prefix_key_values):
    count_of_rows = query_block_rows.shape[0]
    queries_per_group = QUERY_HEADS // KEY_VALUE_HEADS
    query_head_rows = query_block_rows.reshape(count_of_rows, KEY_VALUE_HEADS, queries_per_group, HEAD_SIZE).astype(jnp.float32)
    key_matrix_rows = jnp.concatenate([prefix_key_values[0], suffix_of_block[0]], axis=0).reshape(-1, KEY_VALUE_HEADS, HEAD_SIZE).astype(jnp.float32)
    value_matrix_rows = jnp.concatenate([prefix_key_values[1], suffix_of_block[1]], axis=0).reshape(-1, KEY_VALUE_HEADS, HEAD_SIZE).astype(jnp.float32)
    scores = jnp.einsum('tgjd,rgd->gjtr', query_head_rows, key_matrix_rows, precision=lax.Precision.HIGHEST) * (1.0 / math.sqrt(HEAD_SIZE))
    position = jnp.arange(count_of_rows, dtype=jnp.int32)
    own_visible = (block_ids[:, None] == block_ids[None, :]) & (position[:, None] >= position[None, :])
    visible = jnp.concatenate([jnp.ones((count_of_rows, PREFIX_TOKENS), dtype=jnp.bool_), own_visible], axis=1)
    scores = jnp.where(visible, scores, MASKED_SCORE)
    row_peak = lax.optimization_barrier(jnp.max(scores, axis=3, keepdims=True))
    weights = jnp.exp(scores - row_peak)
    row_total = lax.optimization_barrier(jnp.sum(weights, axis=3))
    rounded_weights = weights.astype(jnp.bfloat16).astype(jnp.float32)
    summed = jnp.einsum('gjtr,rgd->gjtd', rounded_weights, value_matrix_rows, precision=lax.Precision.HIGHEST)
    result = summed / row_total[..., None]
    return jnp.transpose(result, (2, 0, 1, 3)).reshape(count_of_rows, QUERY_HEADS * HEAD_SIZE).astype(jnp.bfloat16)

def reference(residual, queries, suffix_key_values, prefix_key_values, request_ids, out_weight, norm_gain, expert_routes, route_gates, gate_experts, up_experts, down_experts):
    total_in_block = N_REQ * N_EXP
    query_blocks = queries.reshape(total_in_block, DEVICE_TOKENS, D)
    suffix_block_list = jnp.transpose(suffix_key_values.reshape(2, total_in_block, DEVICE_TOKENS, KEY_VALUE_HEADS * HEAD_SIZE), (1, 0, 2, 3))

    def one_block(packed):
        return attend_block(packed[0], packed[1], packed[2], prefix_key_values)
    attended = lax.map(one_block, (query_blocks, suffix_block_list, request_ids)).reshape(SUFFIX_TOKENS, D)
    projected = jnp.dot(attended, out_weight, preferred_element_type=jnp.float32)
    stream = residual.astype(jnp.float32) + projected
    inverse_rms = lax.rsqrt(lax.optimization_barrier(jnp.mean(stream * stream, axis=1, keepdims=True)) + EPSILON)
    normed = (stream * inverse_rms * norm_gain[None, :]).astype(jnp.bfloat16)
    flat_routes = expert_routes.reshape(-1)
    flat_gates = route_gates.reshape(-1)
    slot_total = N_REQ * N_EXP * CAP
    route_index = jnp.arange(SUFFIX_TOKENS * TOP, dtype=jnp.int32)

    def one_expert(accumulated, expert):
        matches = flat_routes == expert
        slot_rank = jnp.cumsum(matches.astype(jnp.int32)) - 1
        slot_of_route = jnp.where(matches, slot_rank, slot_total).astype(jnp.int32)
        sources = jnp.zeros((slot_total,), jnp.int32).at[slot_of_route].set(route_index, mode='drop')
        occupied = jnp.arange(slot_total, dtype=jnp.int32) < jnp.sum(matches.astype(jnp.int32))
        slot_rows = normed[sources // TOP]
        gated = jnp.dot(slot_rows, gate_experts[expert], preferred_element_type=jnp.float32)
        lifted = jnp.dot(slot_rows, up_experts[expert], preferred_element_type=jnp.float32)
        active = (jnp.maximum(gated, 0.0) * lifted).astype(jnp.bfloat16)
        expert_out = jnp.dot(active, down_experts[expert], preferred_element_type=jnp.float32).astype(jnp.bfloat16)
        shares = expert_out.astype(jnp.float32) * jnp.where(occupied, flat_gates[sources], 0.0)[:, None]
        return (accumulated.at[sources // TOP].add(shares), None)
    accumulated, unused = lax.scan(one_expert, jnp.zeros((SUFFIX_TOKENS, D), jnp.float32), jnp.arange(EXPERTS, dtype=jnp.int32))
    return (stream + accumulated).astype(jnp.bfloat16)
```

```python
import math

import jax
import jax.numpy as jnp
from jax import lax
from jax.sharding import PartitionSpec as P
from jax.experimental import pallas as pl
from jax.experimental.pallas import tpu as pltpu

QUERY_HEADS = 12
KEY_VALUE_HEADS = 2
HEAD_SIZE = 128


EPSILON = 1e-06
MASKED_SCORE = -1e30


def attention_kernel(rid_col_ref, rid_row_ref, q_ref, pkv_ref, skv_ref, out_ref):
    local_count = q_ref.shape[0]
    scale = 1.0 / math.sqrt(HEAD_SIZE)
    position = lax.broadcasted_iota(jnp.int32, (local_count, local_count), 0)
    key_position = lax.broadcasted_iota(jnp.int32, (local_count, local_count), 1)
    allowed = (rid_col_ref[...] == rid_row_ref[...]) & (position >= key_position)
    prefix_keys = pkv_ref[0]
    prefix_values = pkv_ref[1]
    suffix_keys = skv_ref[0]
    suffix_values = skv_ref[1]
    contract = (((1,), (1,)), ((), ()))
    for head in range(QUERY_HEADS // KEY_VALUE_HEADS):
        columns = slice(head * HEAD_SIZE, (head + 1) * HEAD_SIZE)
        query_rows = q_ref[:, columns]
        prefix_scores = (
            lax.dot_general(query_rows, prefix_keys, contract, preferred_element_type=jnp.float32)
            * scale
        )
        suffix_scores = (
            lax.dot_general(query_rows, suffix_keys, contract, preferred_element_type=jnp.float32)
            * scale
        )
        suffix_scores = jnp.where(allowed, suffix_scores, MASKED_SCORE)
        peak = jnp.maximum(
            jnp.max(prefix_scores, axis=1, keepdims=True),
            jnp.max(suffix_scores, axis=1, keepdims=True),
        )
        prefix_weights = jnp.exp(prefix_scores - peak)
        suffix_weights = jnp.where(allowed, jnp.exp(suffix_scores - peak), 0.0)
        total = jnp.sum(prefix_weights, axis=1, keepdims=True) + jnp.sum(
            suffix_weights, axis=1, keepdims=True
        )
        summed = jnp.dot(
            prefix_weights.astype(jnp.bfloat16), prefix_values, preferred_element_type=jnp.float32
        ) + jnp.dot(
            suffix_weights.astype(jnp.bfloat16), suffix_values, preferred_element_type=jnp.float32
        )
        out_ref[:, columns] = (summed / total).astype(out_ref.dtype)


def attend(queries, prefix_key_values, suffix_key_values, request_ids):
    local_count, model_width = queries.shape
    prefix_count = prefix_key_values.shape[1]
    group_width = model_width // KEY_VALUE_HEADS
    return pl.pallas_call(
        attention_kernel,
        grid=(KEY_VALUE_HEADS,),
        in_specs=[
            pl.BlockSpec((local_count, 1), lambda g: (0, 0)),
            pl.BlockSpec((1, local_count), lambda g: (0, 0)),
            pl.BlockSpec((local_count, group_width), lambda g: (0, g)),
            pl.BlockSpec((2, prefix_count, HEAD_SIZE), lambda g: (0, 0, g)),
            pl.BlockSpec((2, local_count, HEAD_SIZE), lambda g: (0, 0, g)),
        ],
        out_specs=pl.BlockSpec((local_count, group_width), lambda g: (0, g)),
        out_shape=jax.ShapeDtypeStruct((local_count, model_width), jnp.bfloat16),
        compiler_params=pltpu.CompilerParams(vmem_limit_bytes=48 * 1024 * 1024),
    )(request_ids.reshape(local_count, 1), request_ids.reshape(1, local_count), queries,
      prefix_key_values, suffix_key_values)


def on_device(
    residual,
    queries,
    suffix_key_values,
    prefix_key_values,
    request_ids,
    out_weight,
    norm_gain,
    expert_routes,
    route_gates,
    gate_experts,
    up_experts,
    down_experts,
):
    local_count = queries.shape[0]
    model_width = queries.shape[1]
    exp_count = lax.axis_size("exp")
    by_req = lax.all_gather(prefix_key_values, "req", axis=1, tiled=True)
    spread = jnp.broadcast_to(by_req[:, None], (2, exp_count) + by_req.shape[1:])
    gathered = lax.all_to_all(spread, "exp", split_axis=1, concat_axis=1, tiled=True)
    all_prefix = gathered.reshape(2, exp_count * by_req.shape[1], by_req.shape[2])
    attended = attend(queries, all_prefix, suffix_key_values, request_ids)
    section = attended
    projected = jnp.dot(
        section,
        lax.all_gather(out_weight, "req", axis=0, tiled=True),
        preferred_element_type=jnp.float32,
    )
    stream = residual.astype(jnp.float32) + projected
    inverse_rms = lax.rsqrt(jnp.mean(stream * stream, axis=1, keepdims=True) + EPSILON)
    normed = (stream * inverse_rms * norm_gain[None, :]).astype(jnp.bfloat16)
    top_count = expert_routes.shape[1]
    expert_count = gate_experts.shape[0] * lax.axis_size("exp")
    capacity = 3 * top_count * local_count // (2 * expert_count)
    flat_routes = expert_routes.reshape(-1)
    matches = (flat_routes[:, None] == jnp.arange(expert_count, dtype=jnp.int32)[None, :]).astype(
        jnp.int32
    )
    slot_rank = jnp.sum((jnp.cumsum(matches, axis=0) - 1) * matches, axis=1)
    slot_of_route = flat_routes * capacity + slot_rank
    route_index = jnp.arange(flat_routes.shape[0], dtype=jnp.int32)
    sources = (
        jnp.zeros((expert_count * capacity,), jnp.int32)
        .at[slot_of_route]
        .set(route_index // top_count)
    )
    filled = jnp.zeros((expert_count * capacity,), jnp.bool_).at[slot_of_route].set(True)
    outgoing = jnp.where(filled[:, None], normed[sources], jnp.zeros((), jnp.bfloat16)).reshape(
        expert_count, capacity, model_width
    )
    slot_rows = lax.all_to_all(outgoing, "exp", split_axis=0, concat_axis=0, tiled=True)
    senders, slot_count, features = slot_rows.shape
    flat_rows = slot_rows.reshape(senders * slot_count, features)
    gated = jnp.dot(flat_rows, gate_experts[0], preferred_element_type=jnp.float32)
    lifted = jnp.dot(flat_rows, up_experts[0], preferred_element_type=jnp.float32)
    active = (jnp.maximum(gated, 0.0) * lifted).astype(jnp.bfloat16)
    produced = jnp.dot(active, down_experts[0], preferred_element_type=jnp.float32).astype(
        jnp.bfloat16
    )
    computed = produced.reshape(senders, slot_count, features)
    returned = lax.all_to_all(computed, "exp", split_axis=0, concat_axis=0, tiled=True)
    picked = returned.reshape(expert_count * capacity, model_width)[slot_of_route].reshape(
        local_count, top_count, model_width
    )
    combined = jnp.sum(picked.astype(jnp.float32) * route_gates[:, :, None], axis=1)
    return (stream + combined).astype(jnp.bfloat16)


def solution(mesh):
    placed = (
        P(("req", "exp"), None),
        P(("req", "exp"), None),
        P(None, ("req", "exp"), None),
        P(None, ("req", "exp"), None),
        P(("req", "exp"), None),
        P("req", None),
        P(),
        P(("req", "exp"), None),
        P(("req", "exp"), None),
        P("exp", None, None),
        P("exp", None, None),
        P("exp", None, None),
    )
    return jax.shard_map(
        on_device, mesh=mesh, in_specs=placed, out_specs=P(("req", "exp"), None), check_vma=False
    )
```

```python
import math

import jax
import jax.numpy as jnp
from jax import lax
from jax.sharding import PartitionSpec as P
from jax.experimental import pallas as pl
from jax.experimental.pallas import tpu as pltpu

QUERY_HEADS = 12
KEY_VALUE_HEADS = 2
HEAD_SIZE = 128


EPSILON = 1e-06
MASKED_SCORE = -1e30


def attention_kernel(rid_col_ref, rid_row_ref, q_ref, pkv_ref, skv_ref, out_ref):
    local_count = q_ref.shape[0]
    scale = 1.0 / math.sqrt(HEAD_SIZE)
    position = lax.broadcasted_iota(jnp.int32, (local_count, local_count), 0)
    key_position = lax.broadcasted_iota(jnp.int32, (local_count, local_count), 1)
    allowed = (rid_col_ref[...] == rid_row_ref[...]) & (position >= key_position)
    prefix_keys = pkv_ref[0]
    prefix_values = pkv_ref[1]
    suffix_keys = skv_ref[0]
    suffix_values = skv_ref[1]
    contract = (((1,), (1,)), ((), ()))
    for head in range(QUERY_HEADS // KEY_VALUE_HEADS):
        columns = slice(head * HEAD_SIZE, (head + 1) * HEAD_SIZE)
        query_rows = q_ref[:, columns]
        prefix_scores = (
            lax.dot_general(query_rows, prefix_keys, contract, preferred_element_type=jnp.float32)
            * scale
        )
        suffix_scores = (
            lax.dot_general(query_rows, suffix_keys, contract, preferred_element_type=jnp.float32)
            * scale
        )
        suffix_scores = jnp.where(allowed, suffix_scores, MASKED_SCORE)
        peak = jnp.maximum(
            jnp.max(prefix_scores, axis=1, keepdims=True),
            jnp.max(suffix_scores, axis=1, keepdims=True),
        )
        prefix_weights = jnp.exp(prefix_scores - peak)
        suffix_weights = jnp.where(allowed, jnp.exp(suffix_scores - peak), 0.0)
        total = jnp.sum(prefix_weights, axis=1, keepdims=True) + jnp.sum(
            suffix_weights, axis=1, keepdims=True
        )
        summed = jnp.dot(
            prefix_weights.astype(jnp.bfloat16), prefix_values, preferred_element_type=jnp.float32
        ) + jnp.dot(
            suffix_weights.astype(jnp.bfloat16), suffix_values, preferred_element_type=jnp.float32
        )
        out_ref[:, columns] = (summed / total).astype(out_ref.dtype)


def attend(queries, prefix_key_values, suffix_key_values, request_ids):
    local_count, model_width = queries.shape
    prefix_count = prefix_key_values.shape[1]
    group_width = model_width // KEY_VALUE_HEADS
    return pl.pallas_call(
        attention_kernel,
        grid=(KEY_VALUE_HEADS,),
        in_specs=[
            pl.BlockSpec((local_count, 1), lambda g: (0, 0)),
            pl.BlockSpec((1, local_count), lambda g: (0, 0)),
            pl.BlockSpec((local_count, group_width), lambda g: (0, g)),
            pl.BlockSpec((2, prefix_count, HEAD_SIZE), lambda g: (0, 0, g)),
            pl.BlockSpec((2, local_count, HEAD_SIZE), lambda g: (0, 0, g)),
        ],
        out_specs=pl.BlockSpec((local_count, group_width), lambda g: (0, g)),
        out_shape=jax.ShapeDtypeStruct((local_count, model_width), jnp.bfloat16),
        compiler_params=pltpu.CompilerParams(vmem_limit_bytes=48 * 1024 * 1024),
    )(request_ids.reshape(local_count, 1), request_ids.reshape(1, local_count), queries,
      prefix_key_values, suffix_key_values)


def on_device(
    residual,
    queries,
    suffix_key_values,
    prefix_key_values,
    request_ids,
    out_weight,
    norm_gain,
    expert_routes,
    route_gates,
    gate_experts,
    up_experts,
    down_experts,
):
    local_count = queries.shape[0]
    model_width = queries.shape[1]
    exp_count = lax.axis_size("exp")
    req_count = lax.axis_size("req")
    by_req = lax.all_to_all(
        jnp.broadcast_to(prefix_key_values[:, None], (2, req_count) + prefix_key_values.shape[1:]),
        "req",
        split_axis=1,
        concat_axis=1,
        tiled=True,
    ).reshape(2, req_count * prefix_key_values.shape[1], prefix_key_values.shape[2])
    spread = jnp.broadcast_to(by_req[:, None], (2, exp_count) + by_req.shape[1:])
    gathered = lax.all_to_all(spread, "exp", split_axis=1, concat_axis=1, tiled=True)
    all_prefix = gathered.reshape(2, exp_count * by_req.shape[1], by_req.shape[2])
    attended = attend(queries, all_prefix, suffix_key_values, request_ids)
    section = attended
    projected = jnp.dot(
        section,
        lax.all_gather(out_weight, "req", axis=0, tiled=True),
        preferred_element_type=jnp.float32,
    )
    stream = residual.astype(jnp.float32) + projected
    inverse_rms = lax.rsqrt(jnp.mean(stream * stream, axis=1, keepdims=True) + EPSILON)
    normed = (stream * inverse_rms * norm_gain[None, :]).astype(jnp.bfloat16)
    top_count = expert_routes.shape[1]
    expert_count = gate_experts.shape[0] * lax.axis_size("exp")
    capacity = 3 * top_count * local_count // (2 * expert_count)
    flat_routes = expert_routes.reshape(-1)
    matches = (flat_routes[:, None] == jnp.arange(expert_count, dtype=jnp.int32)[None, :]).astype(
        jnp.int32
    )
    slot_rank = jnp.sum((jnp.cumsum(matches, axis=0) - 1) * matches, axis=1)
    slot_of_route = flat_routes * capacity + slot_rank
    slot_ids = jnp.arange(expert_count * capacity, dtype=jnp.int32)
    hit = slot_of_route.reshape(local_count, top_count)[:, :, None] == slot_ids[None, None, :]
    dispatch = jnp.any(hit, axis=1).astype(jnp.bfloat16)
    outgoing = (
        jnp.einsum("ts,tf->sf", dispatch, normed, preferred_element_type=jnp.float32)
        .astype(jnp.bfloat16)
        .reshape(expert_count, capacity, model_width)
    )
    slot_rows = lax.all_to_all(outgoing, "exp", split_axis=0, concat_axis=0, tiled=True)
    senders, slot_count, features = slot_rows.shape
    flat_rows = slot_rows.reshape(senders * slot_count, features)
    gated = jnp.dot(flat_rows, gate_experts[0], preferred_element_type=jnp.float32)
    lifted = jnp.dot(flat_rows, up_experts[0], preferred_element_type=jnp.float32)
    active = (jnp.maximum(gated, 0.0) * lifted).astype(jnp.bfloat16)
    produced = jnp.dot(active, down_experts[0], preferred_element_type=jnp.float32).astype(
        jnp.bfloat16
    )
    computed = produced.reshape(senders, slot_count, features)
    returned = lax.all_to_all(computed, "exp", split_axis=0, concat_axis=0, tiled=True)
    slot_gates = jnp.sum(jnp.where(hit, route_gates[:, :, None], 0.0), axis=1)
    combined = jnp.dot(
        slot_gates,
        returned.reshape(expert_count * capacity, model_width).astype(jnp.float32),
        precision=lax.Precision.HIGHEST,
        preferred_element_type=jnp.float32,
    )
    return (stream + combined).astype(jnp.bfloat16)


def solution(mesh):
    placed = (
        P(("req", "exp"), None),
        P(("req", "exp"), None),
        P(None, ("req", "exp"), None),
        P(None, ("req", "exp"), None),
        P(("req", "exp"), None),
        P("req", None),
        P(),
        P(("req", "exp"), None),
        P(("req", "exp"), None),
        P("exp", None, None),
        P("exp", None, None),
        P("exp", None, None),
    )
    return jax.shard_map(
        on_device, mesh=mesh, in_specs=placed, out_specs=P(("req", "exp"), None), check_vma=False
    )
```

```python
import math

import jax
import jax.numpy as jnp
from jax import lax
from jax.sharding import Mesh, PartitionSpec as P
from jax.experimental import pallas as pl
from jax.experimental.pallas import tpu as pltpu

QUERY_HEADS = 12
KEY_VALUE_HEADS = 2
HEAD_SIZE = 128


EPSILON = 1e-06
MASKED_SCORE = -1e30
EXP = ("chip", "core")


def attention_kernel(rid_col_ref, rid_row_ref, q_ref, pkv_ref, skv_ref, out_ref):
    local_count = q_ref.shape[0]
    scale = 1.0 / math.sqrt(HEAD_SIZE)
    position = lax.broadcasted_iota(jnp.int32, (local_count, local_count), 0)
    key_position = lax.broadcasted_iota(jnp.int32, (local_count, local_count), 1)
    allowed = (rid_col_ref[...] == rid_row_ref[...]) & (position >= key_position)
    prefix_keys = pkv_ref[0]
    prefix_values = pkv_ref[1]
    suffix_keys = skv_ref[0]
    suffix_values = skv_ref[1]
    contract = (((1,), (1,)), ((), ()))
    for head in range(QUERY_HEADS // KEY_VALUE_HEADS):
        columns = slice(head * HEAD_SIZE, (head + 1) * HEAD_SIZE)
        query_rows = q_ref[:, columns]
        prefix_scores = (
            lax.dot_general(query_rows, prefix_keys, contract, preferred_element_type=jnp.float32)
            * scale
        )
        suffix_scores = (
            lax.dot_general(query_rows, suffix_keys, contract, preferred_element_type=jnp.float32)
            * scale
        )
        suffix_scores = jnp.where(allowed, suffix_scores, MASKED_SCORE)
        peak = jnp.maximum(
            jnp.max(prefix_scores, axis=1, keepdims=True),
            jnp.max(suffix_scores, axis=1, keepdims=True),
        )
        prefix_weights = jnp.exp(prefix_scores - peak)
        suffix_weights = jnp.where(allowed, jnp.exp(suffix_scores - peak), 0.0)
        total = jnp.sum(prefix_weights, axis=1, keepdims=True) + jnp.sum(
            suffix_weights, axis=1, keepdims=True
        )
        summed = jnp.dot(
            prefix_weights.astype(jnp.bfloat16), prefix_values, preferred_element_type=jnp.float32
        ) + jnp.dot(
            suffix_weights.astype(jnp.bfloat16), suffix_values, preferred_element_type=jnp.float32
        )
        out_ref[:, columns] = (summed / total).astype(out_ref.dtype)


def attend(queries, prefix_key_values, suffix_key_values, request_ids):
    local_count, model_width = queries.shape
    prefix_count = prefix_key_values.shape[1]
    group_width = model_width // KEY_VALUE_HEADS
    return pl.pallas_call(
        attention_kernel,
        grid=(KEY_VALUE_HEADS,),
        in_specs=[
            pl.BlockSpec((local_count, 1), lambda g: (0, 0)),
            pl.BlockSpec((1, local_count), lambda g: (0, 0)),
            pl.BlockSpec((local_count, group_width), lambda g: (0, g)),
            pl.BlockSpec((2, prefix_count, HEAD_SIZE), lambda g: (0, 0, g)),
            pl.BlockSpec((2, local_count, HEAD_SIZE), lambda g: (0, 0, g)),
        ],
        out_specs=pl.BlockSpec((local_count, group_width), lambda g: (0, g)),
        out_shape=jax.ShapeDtypeStruct((local_count, model_width), jnp.bfloat16),
        compiler_params=pltpu.CompilerParams(vmem_limit_bytes=48 * 1024 * 1024),
    )(request_ids.reshape(local_count, 1), request_ids.reshape(1, local_count), queries,
      prefix_key_values, suffix_key_values)


def on_device(
    residual,
    queries,
    suffix_key_values,
    prefix_key_values,
    request_ids,
    out_weight,
    norm_gain,
    expert_routes,
    route_gates,
    gate_experts,
    up_experts,
    down_experts,
):
    local_count = queries.shape[0]
    model_width = queries.shape[1]
    chip_count = lax.axis_size("chip")
    core_count = lax.axis_size("core")
    req_count = lax.axis_size("req")
    by_req = lax.all_to_all(
        jnp.broadcast_to(prefix_key_values[:, None], (2, req_count) + prefix_key_values.shape[1:]),
        "req",
        split_axis=1,
        concat_axis=1,
        tiled=True,
    ).reshape(2, req_count * prefix_key_values.shape[1], prefix_key_values.shape[2])
    spread = jnp.broadcast_to(by_req[:, None], (2, chip_count) + by_req.shape[1:])
    by_chip = lax.all_to_all(spread, "chip", split_axis=1, concat_axis=1, tiled=True).reshape(
        2, chip_count * by_req.shape[1], by_req.shape[2]
    )
    paired = jnp.broadcast_to(by_chip[:, None], (2, core_count) + by_chip.shape[1:])
    all_prefix = lax.all_to_all(paired, "core", split_axis=1, concat_axis=1, tiled=True).reshape(
        2, core_count * by_chip.shape[1], by_chip.shape[2]
    )
    attended = attend(queries, all_prefix, suffix_key_values, request_ids)
    section = attended
    projected = jnp.dot(
        section,
        lax.all_gather(out_weight, "req", axis=0, tiled=True),
        preferred_element_type=jnp.float32,
    )
    stream = residual.astype(jnp.float32) + projected
    inverse_rms = lax.rsqrt(jnp.mean(stream * stream, axis=1, keepdims=True) + EPSILON)
    normed = (stream * inverse_rms * norm_gain[None, :]).astype(jnp.bfloat16)
    top_count = expert_routes.shape[1]
    expert_count = gate_experts.shape[0] * lax.axis_size(EXP)
    capacity = 3 * top_count * local_count // (2 * expert_count)
    flat_routes = expert_routes.reshape(-1)
    matches = (flat_routes[:, None] == jnp.arange(expert_count, dtype=jnp.int32)[None, :]).astype(
        jnp.int32
    )
    slot_rank = jnp.sum((jnp.cumsum(matches, axis=0) - 1) * matches, axis=1)
    slot_of_route = flat_routes * capacity + slot_rank
    slot_ids = jnp.arange(expert_count * capacity, dtype=jnp.int32)
    hit = slot_of_route.reshape(local_count, top_count)[:, :, None] == slot_ids[None, None, :]
    dispatch = jnp.any(hit, axis=1).astype(jnp.bfloat16)
    outgoing = (
        jnp.einsum("ts,tf->sf", dispatch, normed, preferred_element_type=jnp.float32)
        .astype(jnp.bfloat16)
        .reshape(expert_count, capacity, model_width)
    )
    slot_rows = lax.all_to_all(outgoing, EXP, split_axis=0, concat_axis=0, tiled=True)
    senders, slot_count, features = slot_rows.shape
    flat_rows = slot_rows.reshape(senders * slot_count, features)
    gated = jnp.dot(flat_rows, gate_experts[0], preferred_element_type=jnp.float32)
    lifted = jnp.dot(flat_rows, up_experts[0], preferred_element_type=jnp.float32)
    active = (jnp.maximum(gated, 0.0) * lifted).astype(jnp.bfloat16)
    produced = jnp.dot(active, down_experts[0], preferred_element_type=jnp.float32).astype(
        jnp.bfloat16
    )
    computed = produced.reshape(senders, slot_count, features)
    returned = lax.all_to_all(computed, EXP, split_axis=0, concat_axis=0, tiled=True)
    slot_gates = jnp.sum(jnp.where(hit, route_gates[:, :, None], 0.0), axis=1)
    combined = jnp.dot(
        slot_gates,
        returned.reshape(expert_count * capacity, model_width).astype(jnp.float32),
        precision=lax.Precision.HIGHEST,
        preferred_element_type=jnp.float32,
    )
    return (stream + combined).astype(jnp.bfloat16)


def solution(mesh):
    placed = (
        P(("req", "chip", "core"), None),
        P(("req", "chip", "core"), None),
        P(None, ("req", "chip", "core"), None),
        P(None, ("req", "chip", "core"), None),
        P(("req", "chip", "core"), None),
        P("req", None),
        P(),
        P(("req", "chip", "core"), None),
        P(("req", "chip", "core"), None),
        P(EXP, None, None),
        P(EXP, None, None),
        P(EXP, None, None),
    )
    req_count, exp_count = mesh.devices.shape
    split_mesh = Mesh(
        mesh.devices.reshape(req_count, exp_count // 2, 2), ("req", "chip", "core")
    )
    return jax.shard_map(
        on_device, mesh=split_mesh, in_specs=placed, out_specs=P(("req", "chip", "core"), None), check_vma=False
    )
```

```python
import math

import jax
import jax.numpy as jnp
from jax import lax
from jax.sharding import Mesh, PartitionSpec as P
from jax.experimental import pallas as pl
from jax.experimental.pallas import tpu as pltpu

QUERY_HEADS = 12
KEY_VALUE_HEADS = 2
HEAD_SIZE = 128


EPSILON = 1e-06
MASKED_SCORE = -1e30
EXP = ("chip", "core")


def attention_kernel(rid_col_ref, rid_row_ref, q_ref, pkv_ref, skv_ref, out_ref):
    local_count = q_ref.shape[0]
    scale = 1.0 / math.sqrt(HEAD_SIZE)
    position = lax.broadcasted_iota(jnp.int32, (local_count, local_count), 0)
    key_position = lax.broadcasted_iota(jnp.int32, (local_count, local_count), 1)
    allowed = (rid_col_ref[...] == rid_row_ref[...]) & (position >= key_position)
    prefix_keys = pkv_ref[0]
    prefix_values = pkv_ref[1]
    suffix_keys = skv_ref[0]
    suffix_values = skv_ref[1]
    contract = (((1,), (1,)), ((), ()))
    for head in range(QUERY_HEADS // KEY_VALUE_HEADS):
        columns = slice(head * HEAD_SIZE, (head + 1) * HEAD_SIZE)
        query_rows = q_ref[:, columns]
        prefix_scores = (
            lax.dot_general(query_rows, prefix_keys, contract, preferred_element_type=jnp.float32)
            * scale
        )
        suffix_scores = (
            lax.dot_general(query_rows, suffix_keys, contract, preferred_element_type=jnp.float32)
            * scale
        )
        suffix_scores = jnp.where(allowed, suffix_scores, MASKED_SCORE)
        peak = jnp.maximum(
            jnp.max(prefix_scores, axis=1, keepdims=True),
            jnp.max(suffix_scores, axis=1, keepdims=True),
        )
        prefix_weights = jnp.exp(prefix_scores - peak)
        suffix_weights = jnp.where(allowed, jnp.exp(suffix_scores - peak), 0.0)
        total = jnp.sum(prefix_weights, axis=1, keepdims=True) + jnp.sum(
            suffix_weights, axis=1, keepdims=True
        )
        summed = jnp.dot(
            prefix_weights.astype(jnp.bfloat16), prefix_values, preferred_element_type=jnp.float32
        ) + jnp.dot(
            suffix_weights.astype(jnp.bfloat16), suffix_values, preferred_element_type=jnp.float32
        )
        out_ref[:, columns] = (summed / total).astype(out_ref.dtype)


def attend(queries, prefix_key_values, suffix_key_values, request_ids):
    local_count, model_width = queries.shape
    prefix_count = prefix_key_values.shape[1]
    group_width = model_width // KEY_VALUE_HEADS
    return pl.pallas_call(
        attention_kernel,
        grid=(KEY_VALUE_HEADS,),
        in_specs=[
            pl.BlockSpec((local_count, 1), lambda g: (0, 0)),
            pl.BlockSpec((1, local_count), lambda g: (0, 0)),
            pl.BlockSpec((local_count, group_width), lambda g: (0, g)),
            pl.BlockSpec((2, prefix_count, HEAD_SIZE), lambda g: (0, 0, g)),
            pl.BlockSpec((2, local_count, HEAD_SIZE), lambda g: (0, 0, g)),
        ],
        out_specs=pl.BlockSpec((local_count, group_width), lambda g: (0, g)),
        out_shape=jax.ShapeDtypeStruct((local_count, model_width), jnp.bfloat16),
        compiler_params=pltpu.CompilerParams(vmem_limit_bytes=48 * 1024 * 1024),
    )(request_ids.reshape(local_count, 1), request_ids.reshape(1, local_count), queries,
      prefix_key_values, suffix_key_values)


def on_device(
    residual,
    queries,
    suffix_key_values,
    prefix_key_values,
    request_ids,
    out_weight,
    norm_gain,
    expert_routes,
    route_gates,
    gate_experts,
    up_experts,
    down_experts,
):
    local_count = queries.shape[0]
    model_width = queries.shape[1]
    chip_count = lax.axis_size("chip")
    core_count = lax.axis_size("core")
    req_count = lax.axis_size("req")
    by_req = lax.all_to_all(
        jnp.broadcast_to(prefix_key_values[:, None], (2, req_count) + prefix_key_values.shape[1:]),
        "req",
        split_axis=1,
        concat_axis=1,
        tiled=True,
    ).reshape(2, req_count * prefix_key_values.shape[1], prefix_key_values.shape[2])
    spread = jnp.broadcast_to(by_req[:, None], (2, chip_count) + by_req.shape[1:])
    by_chip = lax.all_to_all(spread, "chip", split_axis=1, concat_axis=1, tiled=True).reshape(
        2, chip_count * by_req.shape[1], by_req.shape[2]
    )
    paired = jnp.broadcast_to(by_chip[:, None], (2, core_count) + by_chip.shape[1:])
    all_prefix = lax.all_to_all(paired, "core", split_axis=1, concat_axis=1, tiled=True).reshape(
        2, core_count * by_chip.shape[1], by_chip.shape[2]
    )
    attended = attend(queries, all_prefix, suffix_key_values, request_ids)
    section = attended
    projected = jnp.dot(
        section,
        lax.all_gather(out_weight, "req", axis=0, tiled=True),
        preferred_element_type=jnp.float32,
    )
    stream = residual.astype(jnp.float32) + projected
    inverse_rms = lax.rsqrt(jnp.mean(stream * stream, axis=1, keepdims=True) + EPSILON)
    normed = (stream * inverse_rms * norm_gain[None, :]).astype(jnp.bfloat16)
    top_count = expert_routes.shape[1]
    expert_count = gate_experts.shape[0] * lax.axis_size(EXP)
    capacity = 3 * top_count * local_count // (2 * expert_count)
    flat_routes = expert_routes.reshape(-1)
    matches = (flat_routes[:, None] == jnp.arange(expert_count, dtype=jnp.int32)[None, :]).astype(
        jnp.int32
    )
    slot_rank = jnp.sum((jnp.cumsum(matches, axis=0) - 1) * matches, axis=1)
    chunks = 2 if capacity % 2 == 0 else 1
    part = capacity // chunks
    slot_of_route = (
        (slot_rank // part) * (expert_count * part) + flat_routes * part + slot_rank % part
    )
    slot_ids = jnp.arange(expert_count * capacity, dtype=jnp.int32)
    hit = slot_of_route.reshape(local_count, top_count)[:, :, None] == slot_ids[None, None, :]
    dispatch = jnp.any(hit, axis=1).astype(jnp.bfloat16)
    outgoing = (
        jnp.einsum("ts,tf->sf", dispatch, normed, preferred_element_type=jnp.float32)
        .astype(jnp.bfloat16)
        .reshape(chunks, expert_count, part, model_width)
    )
    returned_parts = []
    for chunk in range(chunks):
        slot_rows = lax.all_to_all(outgoing[chunk], EXP, split_axis=0, concat_axis=0, tiled=True)
        senders, slot_count, features = slot_rows.shape
        flat_rows = slot_rows.reshape(senders * slot_count, features)
        gated = jnp.dot(flat_rows, gate_experts[0], preferred_element_type=jnp.float32)
        lifted = jnp.dot(flat_rows, up_experts[0], preferred_element_type=jnp.float32)
        active = (jnp.maximum(gated, 0.0) * lifted).astype(jnp.bfloat16)
        produced = jnp.dot(active, down_experts[0], preferred_element_type=jnp.float32).astype(
            jnp.bfloat16
        )
        computed = produced.reshape(senders, slot_count, features)
        returned_parts.append(
            lax.all_to_all(computed, EXP, split_axis=0, concat_axis=0, tiled=True)
        )
    returned = jnp.stack(returned_parts)
    slot_gates = jnp.sum(jnp.where(hit, route_gates[:, :, None], 0.0), axis=1)
    combined = jnp.dot(
        slot_gates,
        returned.reshape(expert_count * capacity, model_width).astype(jnp.float32),
        precision=lax.Precision.HIGHEST,
        preferred_element_type=jnp.float32,
    )
    return (stream + combined).astype(jnp.bfloat16)


def solution(mesh):
    placed = (
        P(("req", "chip", "core"), None),
        P(("req", "chip", "core"), None),
        P(None, ("req", "chip", "core"), None),
        P(None, ("req", "chip", "core"), None),
        P(("req", "chip", "core"), None),
        P("req", None),
        P(),
        P(("req", "chip", "core"), None),
        P(("req", "chip", "core"), None),
        P(EXP, None, None),
        P(EXP, None, None),
        P(EXP, None, None),
    )
    req_count, exp_count = mesh.devices.shape
    split_mesh = Mesh(
        mesh.devices.reshape(req_count, exp_count // 2, 2), ("req", "chip", "core")
    )
    return jax.shard_map(
        on_device, mesh=split_mesh, in_specs=placed, out_specs=P(("req", "chip", "core"), None), check_vma=False
    )
```

```python
import math

import jax
import jax.numpy as jnp
from jax import lax
from jax.sharding import Mesh, PartitionSpec as P
from jax.experimental import pallas as pl
from jax.experimental.pallas import tpu as pltpu

QUERY_HEADS = 12
KEY_VALUE_HEADS = 2
HEAD_SIZE = 128


EPSILON = 1e-06
MASKED_SCORE = -1e30
EXP = ("chip", "core")


def attention_kernel(rid_col_ref, rid_row_ref, q_ref, pkv_ref, skv_ref, out_ref):
    local_count = q_ref.shape[0]
    scale = 1.0 / math.sqrt(HEAD_SIZE)
    position = lax.broadcasted_iota(jnp.int32, (local_count, local_count), 0)
    key_position = lax.broadcasted_iota(jnp.int32, (local_count, local_count), 1)
    allowed = (rid_col_ref[...] == rid_row_ref[...]) & (position >= key_position)
    prefix_keys = pkv_ref[0]
    prefix_values = pkv_ref[1]
    suffix_keys = skv_ref[0]
    suffix_values = skv_ref[1]
    contract = (((1,), (1,)), ((), ()))
    for head in range(QUERY_HEADS // KEY_VALUE_HEADS):
        columns = slice(head * HEAD_SIZE, (head + 1) * HEAD_SIZE)
        query_rows = q_ref[:, columns]
        prefix_scores = (
            lax.dot_general(query_rows, prefix_keys, contract, preferred_element_type=jnp.float32)
            * scale
        )
        suffix_scores = (
            lax.dot_general(query_rows, suffix_keys, contract, preferred_element_type=jnp.float32)
            * scale
        )
        suffix_scores = jnp.where(allowed, suffix_scores, MASKED_SCORE)
        peak = jnp.maximum(
            jnp.max(prefix_scores, axis=1, keepdims=True),
            jnp.max(suffix_scores, axis=1, keepdims=True),
        )
        prefix_weights = jnp.exp(prefix_scores - peak)
        suffix_weights = jnp.where(allowed, jnp.exp(suffix_scores - peak), 0.0)
        total = jnp.sum(prefix_weights, axis=1, keepdims=True) + jnp.sum(
            suffix_weights, axis=1, keepdims=True
        )
        summed = jnp.dot(
            prefix_weights.astype(jnp.bfloat16), prefix_values, preferred_element_type=jnp.float32
        ) + jnp.dot(
            suffix_weights.astype(jnp.bfloat16), suffix_values, preferred_element_type=jnp.float32
        )
        out_ref[:, columns] = (summed / total).astype(out_ref.dtype)


def attend(queries, prefix_key_values, suffix_key_values, request_ids):
    local_count, model_width = queries.shape
    prefix_count = prefix_key_values.shape[1]
    group_width = model_width // KEY_VALUE_HEADS
    return pl.pallas_call(
        attention_kernel,
        grid=(KEY_VALUE_HEADS,),
        in_specs=[
            pl.BlockSpec((local_count, 1), lambda g: (0, 0)),
            pl.BlockSpec((1, local_count), lambda g: (0, 0)),
            pl.BlockSpec((local_count, group_width), lambda g: (0, g)),
            pl.BlockSpec((2, prefix_count, HEAD_SIZE), lambda g: (0, 0, g)),
            pl.BlockSpec((2, local_count, HEAD_SIZE), lambda g: (0, 0, g)),
        ],
        out_specs=pl.BlockSpec((local_count, group_width), lambda g: (0, g)),
        out_shape=jax.ShapeDtypeStruct((local_count, model_width), jnp.bfloat16),
        compiler_params=pltpu.CompilerParams(vmem_limit_bytes=48 * 1024 * 1024),
    )(request_ids.reshape(local_count, 1), request_ids.reshape(1, local_count), queries,
      prefix_key_values, suffix_key_values)


def expert_kernel(rows_ref, gate_ref, up_ref, down_ref, out_ref, acc_ref):
    step = pl.program_id(0)

    @pl.when(step == 0)
    def _():
        acc_ref[...] = jnp.zeros_like(acc_ref)

    rows = rows_ref[...]
    gated = jnp.dot(rows, gate_ref[...], preferred_element_type=jnp.float32)
    lifted = jnp.dot(rows, up_ref[...], preferred_element_type=jnp.float32)
    active = (jnp.maximum(gated, 0.0) * lifted).astype(jnp.bfloat16)
    acc_ref[...] += jnp.dot(active, down_ref[...], preferred_element_type=jnp.float32)

    @pl.when(step == pl.num_programs(0) - 1)
    def _():
        out_ref[...] = acc_ref[...].astype(out_ref.dtype)


def expert_ffn(rows, gate_experts, up_experts, down_experts):
    count, width = rows.shape
    hidden = gate_experts.shape[2]
    block = 256 if hidden % 256 == 0 else hidden
    return pl.pallas_call(
        expert_kernel,
        grid=(hidden // block,),
        in_specs=[
            pl.BlockSpec((count, width), lambda f: (0, 0)),
            pl.BlockSpec((None, width, block), lambda f: (0, 0, f)),
            pl.BlockSpec((None, width, block), lambda f: (0, 0, f)),
            pl.BlockSpec((None, block, width), lambda f: (0, f, 0)),
        ],
        out_specs=pl.BlockSpec((count, width), lambda f: (0, 0)),
        out_shape=jax.ShapeDtypeStruct((count, width), jnp.bfloat16),
        scratch_shapes=[pltpu.VMEM((count, width), jnp.float32)],
        compiler_params=pltpu.CompilerParams(vmem_limit_bytes=48 * 1024 * 1024),
    )(rows, gate_experts, up_experts, down_experts)


def on_device(
    residual,
    queries,
    suffix_key_values,
    prefix_key_values,
    request_ids,
    out_weight,
    norm_gain,
    expert_routes,
    route_gates,
    gate_experts,
    up_experts,
    down_experts,
):
    local_count = queries.shape[0]
    model_width = queries.shape[1]
    chip_count = lax.axis_size("chip")
    core_count = lax.axis_size("core")
    req_count = lax.axis_size("req")
    by_req = lax.all_to_all(
        jnp.broadcast_to(prefix_key_values[:, None], (2, req_count) + prefix_key_values.shape[1:]),
        "req",
        split_axis=1,
        concat_axis=1,
        tiled=True,
    ).reshape(2, req_count * prefix_key_values.shape[1], prefix_key_values.shape[2])
    spread = jnp.broadcast_to(by_req[:, None], (2, chip_count) + by_req.shape[1:])
    by_chip = lax.all_to_all(spread, "chip", split_axis=1, concat_axis=1, tiled=True).reshape(
        2, chip_count * by_req.shape[1], by_req.shape[2]
    )
    paired = jnp.broadcast_to(by_chip[:, None], (2, core_count) + by_chip.shape[1:])
    all_prefix = lax.all_to_all(paired, "core", split_axis=1, concat_axis=1, tiled=True).reshape(
        2, core_count * by_chip.shape[1], by_chip.shape[2]
    )
    attended = attend(queries, all_prefix, suffix_key_values, request_ids)
    section = attended
    projected = jnp.dot(
        section,
        lax.all_gather(out_weight, "req", axis=0, tiled=True),
        preferred_element_type=jnp.float32,
    )
    stream = residual.astype(jnp.float32) + projected
    inverse_rms = lax.rsqrt(jnp.mean(stream * stream, axis=1, keepdims=True) + EPSILON)
    normed = (stream * inverse_rms * norm_gain[None, :]).astype(jnp.bfloat16)
    top_count = expert_routes.shape[1]
    expert_count = gate_experts.shape[0] * lax.axis_size(EXP)
    capacity = 3 * top_count * local_count // (2 * expert_count)
    flat_routes = expert_routes.reshape(-1)
    matches = (flat_routes[:, None] == jnp.arange(expert_count, dtype=jnp.int32)[None, :]).astype(
        jnp.int32
    )
    slot_rank = jnp.sum((jnp.cumsum(matches, axis=0) - 1) * matches, axis=1)
    slot_of_route = flat_routes * capacity + slot_rank
    slot_ids = jnp.arange(expert_count * capacity, dtype=jnp.int32)
    hit = slot_of_route.reshape(local_count, top_count)[:, :, None] == slot_ids[None, None, :]
    dispatch = jnp.any(hit, axis=1).astype(jnp.bfloat16)
    outgoing = (
        jnp.einsum("ts,tf->sf", dispatch, normed, preferred_element_type=jnp.float32)
        .astype(jnp.bfloat16)
        .reshape(expert_count, capacity, model_width)
    )
    slot_rows = lax.all_to_all(outgoing, EXP, split_axis=0, concat_axis=0, tiled=True)
    senders, slot_count, features = slot_rows.shape
    flat_rows = slot_rows.reshape(senders * slot_count, features)
    produced = expert_ffn(flat_rows, gate_experts, up_experts, down_experts)
    computed = produced.reshape(senders, slot_count, features)
    returned = lax.all_to_all(computed, EXP, split_axis=0, concat_axis=0, tiled=True)
    slot_gates = jnp.sum(jnp.where(hit, route_gates[:, :, None], 0.0), axis=1)
    combined = jnp.dot(
        slot_gates,
        returned.reshape(expert_count * capacity, model_width).astype(jnp.float32),
        precision=lax.Precision.HIGHEST,
        preferred_element_type=jnp.float32,
    )
    return (stream + combined).astype(jnp.bfloat16)


def solution(mesh):
    placed = (
        P(("req", "chip", "core"), None),
        P(("req", "chip", "core"), None),
        P(None, ("req", "chip", "core"), None),
        P(None, ("req", "chip", "core"), None),
        P(("req", "chip", "core"), None),
        P("req", None),
        P(),
        P(("req", "chip", "core"), None),
        P(("req", "chip", "core"), None),
        P(EXP, None, None),
        P(EXP, None, None),
        P(EXP, None, None),
    )
    req_count, exp_count = mesh.devices.shape
    split_mesh = Mesh(
        mesh.devices.reshape(req_count, exp_count // 2, 2), ("req", "chip", "core")
    )
    return jax.shard_map(
        on_device, mesh=split_mesh, in_specs=placed, out_specs=P(("req", "chip", "core"), None), check_vma=False
    )
```

```python
import math

import jax
import jax.numpy as jnp
from jax import lax
from jax.sharding import Mesh, PartitionSpec as P
from jax.experimental import pallas as pl
from jax.experimental.pallas import tpu as pltpu

QUERY_HEADS = 12
KEY_VALUE_HEADS = 2
HEAD_SIZE = 128


EPSILON = 1e-06
MASKED_SCORE = -1e30
EXP = ("chip", "core")


def head_scores(q_ref, keys, head):
    columns = slice(head * HEAD_SIZE, (head + 1) * HEAD_SIZE)
    contract = (((1,), (1,)), ((), ()))
    return lax.dot_general(
        q_ref[:, columns], keys, contract, preferred_element_type=jnp.float32
    ) * (1.0 / math.sqrt(HEAD_SIZE))


def local_kernel(rid_col_ref, rid_row_ref, q_ref, pkv_ref, skv_ref, acc_ref, peak_ref, total_ref):
    local_count = q_ref.shape[0]
    position = lax.broadcasted_iota(jnp.int32, (local_count, local_count), 0)
    key_position = lax.broadcasted_iota(jnp.int32, (local_count, local_count), 1)
    allowed = (rid_col_ref[...] == rid_row_ref[...]) & (position >= key_position)
    groups = QUERY_HEADS // KEY_VALUE_HEADS
    for head in range(QUERY_HEADS):
        kv_columns = slice((head // groups) * HEAD_SIZE, (head // groups + 1) * HEAD_SIZE)
        columns = slice(head * HEAD_SIZE, (head + 1) * HEAD_SIZE)
        prefix_scores = head_scores(q_ref, pkv_ref[0, :, kv_columns], head)
        suffix_scores = head_scores(q_ref, skv_ref[0, :, kv_columns], head)
        suffix_scores = jnp.where(allowed, suffix_scores, MASKED_SCORE)
        peak = jnp.maximum(
            jnp.max(prefix_scores, axis=1, keepdims=True),
            jnp.max(suffix_scores, axis=1, keepdims=True),
        )
        prefix_weights = jnp.exp(prefix_scores - peak)
        suffix_weights = jnp.where(allowed, jnp.exp(suffix_scores - peak), 0.0)
        total_ref[:, head : head + 1] = jnp.sum(prefix_weights, axis=1, keepdims=True) + jnp.sum(
            suffix_weights, axis=1, keepdims=True
        )
        peak_ref[:, head : head + 1] = peak
        acc_ref[:, columns] = jnp.dot(
            prefix_weights.astype(jnp.bfloat16),
            pkv_ref[1, :, kv_columns],
            preferred_element_type=jnp.float32,
        ) + jnp.dot(
            suffix_weights.astype(jnp.bfloat16),
            skv_ref[1, :, kv_columns],
            preferred_element_type=jnp.float32,
        )


def merge_kernel(q_ref, pkv_ref, acc_ref, peak_ref, total_ref, out_ref):
    groups = QUERY_HEADS // KEY_VALUE_HEADS
    for head in range(QUERY_HEADS):
        kv_columns = slice((head // groups) * HEAD_SIZE, (head // groups + 1) * HEAD_SIZE)
        columns = slice(head * HEAD_SIZE, (head + 1) * HEAD_SIZE)
        scores = head_scores(q_ref, pkv_ref[0, :, kv_columns], head)
        own_peak = jnp.max(scores, axis=1, keepdims=True)
        weights = jnp.exp(scores - own_peak)
        own_total = jnp.sum(weights, axis=1, keepdims=True)
        own_acc = jnp.dot(
            weights.astype(jnp.bfloat16), pkv_ref[1, :, kv_columns], preferred_element_type=jnp.float32
        )
        first_peak = peak_ref[:, head : head + 1]
        peak = jnp.maximum(first_peak, own_peak)
        first_scale = jnp.exp(first_peak - peak)
        own_scale = jnp.exp(own_peak - peak)
        total = total_ref[:, head : head + 1] * first_scale + own_total * own_scale
        summed = acc_ref[:, columns] * first_scale + own_acc * own_scale
        out_ref[:, columns] = (summed / total).astype(out_ref.dtype)


def whole(shape):
    return pl.BlockSpec(shape, lambda: (0,) * len(shape))


def attend_local(queries, prefix_key_values, suffix_key_values, request_ids):
    local_count, model_width = queries.shape
    column, row = request_ids.reshape(local_count, 1), request_ids.reshape(1, local_count)
    inputs = (column, row, queries, prefix_key_values, suffix_key_values)
    stats = jax.ShapeDtypeStruct((local_count, QUERY_HEADS), jnp.float32)
    return pl.pallas_call(
        local_kernel,
        in_specs=[whole(x.shape) for x in inputs],
        out_specs=[whole((local_count, model_width)), whole(stats.shape), whole(stats.shape)],
        out_shape=[jax.ShapeDtypeStruct((local_count, model_width), jnp.float32), stats, stats],
        compiler_params=pltpu.CompilerParams(vmem_limit_bytes=48 * 1024 * 1024),
    )(*inputs)


def attend_merge(queries, prefix_key_values, acc, peak, total):
    inputs = (queries, prefix_key_values, acc, peak, total)
    return pl.pallas_call(
        merge_kernel,
        in_specs=[whole(x.shape) for x in inputs],
        out_specs=whole(queries.shape),
        out_shape=jax.ShapeDtypeStruct(queries.shape, jnp.bfloat16),
        compiler_params=pltpu.CompilerParams(vmem_limit_bytes=48 * 1024 * 1024),
    )(*inputs)


def expert_kernel(rows_ref, gate_ref, up_ref, down_ref, out_ref, acc_ref):
    step = pl.program_id(0)

    @pl.when(step == 0)
    def _():
        acc_ref[...] = jnp.zeros_like(acc_ref)

    rows = rows_ref[...]
    gated = jnp.dot(rows, gate_ref[...], preferred_element_type=jnp.float32)
    lifted = jnp.dot(rows, up_ref[...], preferred_element_type=jnp.float32)
    active = (jnp.maximum(gated, 0.0) * lifted).astype(jnp.bfloat16)
    acc_ref[...] += jnp.dot(active, down_ref[...], preferred_element_type=jnp.float32)

    @pl.when(step == pl.num_programs(0) - 1)
    def _():
        out_ref[...] = acc_ref[...].astype(out_ref.dtype)


def expert_ffn(rows, gate_experts, up_experts, down_experts):
    count, width = rows.shape
    hidden = gate_experts.shape[2]
    block = 256 if hidden % 256 == 0 else hidden
    return pl.pallas_call(
        expert_kernel,
        grid=(hidden // block,),
        in_specs=[
            pl.BlockSpec((count, width), lambda f: (0, 0)),
            pl.BlockSpec((None, width, block), lambda f: (0, 0, f)),
            pl.BlockSpec((None, width, block), lambda f: (0, 0, f)),
            pl.BlockSpec((None, block, width), lambda f: (0, f, 0)),
        ],
        out_specs=pl.BlockSpec((count, width), lambda f: (0, 0)),
        out_shape=jax.ShapeDtypeStruct((count, width), jnp.bfloat16),
        scratch_shapes=[pltpu.VMEM((count, width), jnp.float32)],
        compiler_params=pltpu.CompilerParams(vmem_limit_bytes=48 * 1024 * 1024),
    )(rows, gate_experts, up_experts, down_experts)


def on_device(
    residual,
    queries,
    suffix_key_values,
    prefix_key_values,
    request_ids,
    out_weight,
    norm_gain,
    expert_routes,
    route_gates,
    gate_experts,
    up_experts,
    down_experts,
):
    local_count = queries.shape[0]
    model_width = queries.shape[1]
    chip_count = lax.axis_size("chip")
    req_count = lax.axis_size("req")
    by_req = lax.all_to_all(
        jnp.broadcast_to(prefix_key_values[:, None], (2, req_count) + prefix_key_values.shape[1:]),
        "req",
        split_axis=1,
        concat_axis=1,
        tiled=True,
    ).reshape(2, req_count * prefix_key_values.shape[1], prefix_key_values.shape[2])
    spread = jnp.broadcast_to(by_req[:, None], (2, chip_count) + by_req.shape[1:])
    by_chip = lax.all_to_all(spread, "chip", split_axis=1, concat_axis=1, tiled=True).reshape(
        2, chip_count * by_req.shape[1], by_req.shape[2]
    )
    partner_half = lax.ppermute(by_chip, "core", [(0, 1), (1, 0)])
    acc, peak, total = attend_local(queries, by_chip, suffix_key_values, request_ids)
    attended = attend_merge(queries, partner_half, acc, peak, total)
    section = attended
    projected = jnp.dot(
        section,
        lax.all_gather(out_weight, "req", axis=0, tiled=True),
        preferred_element_type=jnp.float32,
    )
    stream = residual.astype(jnp.float32) + projected
    inverse_rms = lax.rsqrt(jnp.mean(stream * stream, axis=1, keepdims=True) + EPSILON)
    normed = (stream * inverse_rms * norm_gain[None, :]).astype(jnp.bfloat16)
    top_count = expert_routes.shape[1]
    expert_count = gate_experts.shape[0] * lax.axis_size(EXP)
    capacity = 3 * top_count * local_count // (2 * expert_count)
    flat_routes = expert_routes.reshape(-1)
    matches = (flat_routes[:, None] == jnp.arange(expert_count, dtype=jnp.int32)[None, :]).astype(
        jnp.int32
    )
    slot_rank = jnp.sum((jnp.cumsum(matches, axis=0) - 1) * matches, axis=1)
    slot_of_route = flat_routes * capacity + slot_rank
    slot_ids = jnp.arange(expert_count * capacity, dtype=jnp.int32)
    hit = slot_of_route.reshape(local_count, top_count)[:, :, None] == slot_ids[None, None, :]
    dispatch = jnp.any(hit, axis=1).astype(jnp.bfloat16)
    outgoing = (
        jnp.einsum("ts,tf->sf", dispatch, normed, preferred_element_type=jnp.float32)
        .astype(jnp.bfloat16)
        .reshape(expert_count, capacity, model_width)
    )
    slot_rows = lax.all_to_all(outgoing, EXP, split_axis=0, concat_axis=0, tiled=True)
    senders, slot_count, features = slot_rows.shape
    flat_rows = slot_rows.reshape(senders * slot_count, features)
    produced = expert_ffn(flat_rows, gate_experts, up_experts, down_experts)
    computed = produced.reshape(senders, slot_count, features)
    returned = lax.all_to_all(computed, EXP, split_axis=0, concat_axis=0, tiled=True)
    slot_gates = jnp.sum(jnp.where(hit, route_gates[:, :, None], 0.0), axis=1)
    combined = jnp.dot(
        slot_gates,
        returned.reshape(expert_count * capacity, model_width).astype(jnp.float32),
        precision=lax.Precision.HIGHEST,
        preferred_element_type=jnp.float32,
    )
    return (stream + combined).astype(jnp.bfloat16)


def solution(mesh):
    placed = (
        P(("req", "chip", "core"), None),
        P(("req", "chip", "core"), None),
        P(None, ("req", "chip", "core"), None),
        P(None, ("req", "chip", "core"), None),
        P(("req", "chip", "core"), None),
        P("req", None),
        P(),
        P(("req", "chip", "core"), None),
        P(("req", "chip", "core"), None),
        P(EXP, None, None),
        P(EXP, None, None),
        P(EXP, None, None),
    )
    req_count, exp_count = mesh.devices.shape
    split_mesh = Mesh(
        mesh.devices.reshape(req_count, exp_count // 2, 2), ("req", "chip", "core")
    )
    return jax.shard_map(
        on_device, mesh=split_mesh, in_specs=placed, out_specs=P(("req", "chip", "core"), None), check_vma=False
    )
```

```python
import math

import jax
import jax.numpy as jnp
from jax import lax
from jax.sharding import Mesh, PartitionSpec as P
from jax.experimental import pallas as pl
from jax.experimental.pallas import tpu as pltpu

QUERY_HEADS = 12
KEY_VALUE_HEADS = 2
HEAD_SIZE = 128


EPSILON = 1e-06
MASKED_SCORE = -1e30
EXP = ("chip", "core")


def head_scores(q_ref, keys, head):
    columns = slice(head * HEAD_SIZE, (head + 1) * HEAD_SIZE)
    contract = (((1,), (1,)), ((), ()))
    return lax.dot_general(
        q_ref[:, columns], keys, contract, preferred_element_type=jnp.float32
    ) * (1.0 / math.sqrt(HEAD_SIZE))


def local_kernel(rid_col_ref, rid_row_ref, q_ref, pkv_ref, skv_ref, acc_ref, peak_ref, total_ref):
    local_count = q_ref.shape[0]
    position = lax.broadcasted_iota(jnp.int32, (local_count, local_count), 0)
    key_position = lax.broadcasted_iota(jnp.int32, (local_count, local_count), 1)
    allowed = (rid_col_ref[...] == rid_row_ref[...]) & (position >= key_position)
    groups = QUERY_HEADS // KEY_VALUE_HEADS
    for head in range(QUERY_HEADS):
        kv_columns = slice((head // groups) * HEAD_SIZE, (head // groups + 1) * HEAD_SIZE)
        columns = slice(head * HEAD_SIZE, (head + 1) * HEAD_SIZE)
        prefix_scores = head_scores(q_ref, pkv_ref[0, :, kv_columns], head)
        suffix_scores = head_scores(q_ref, skv_ref[0, :, kv_columns], head)
        suffix_scores = jnp.where(allowed, suffix_scores, MASKED_SCORE)
        peak = jnp.maximum(
            jnp.max(prefix_scores, axis=1, keepdims=True),
            jnp.max(suffix_scores, axis=1, keepdims=True),
        )
        prefix_weights = jnp.exp(prefix_scores - peak)
        suffix_weights = jnp.where(allowed, jnp.exp(suffix_scores - peak), 0.0)
        total_ref[:, head : head + 1] = jnp.sum(prefix_weights, axis=1, keepdims=True) + jnp.sum(
            suffix_weights, axis=1, keepdims=True
        )
        peak_ref[:, head : head + 1] = peak
        acc_ref[:, columns] = jnp.dot(
            prefix_weights.astype(jnp.bfloat16),
            pkv_ref[1, :, kv_columns],
            preferred_element_type=jnp.float32,
        ) + jnp.dot(
            suffix_weights.astype(jnp.bfloat16),
            skv_ref[1, :, kv_columns],
            preferred_element_type=jnp.float32,
        )


def merge_kernel(q_ref, pkv_ref, acc_ref, peak_ref, total_ref, out_ref):
    groups = QUERY_HEADS // KEY_VALUE_HEADS
    for head in range(QUERY_HEADS):
        kv_columns = slice((head // groups) * HEAD_SIZE, (head // groups + 1) * HEAD_SIZE)
        columns = slice(head * HEAD_SIZE, (head + 1) * HEAD_SIZE)
        scores = head_scores(q_ref, pkv_ref[0, :, kv_columns], head)
        own_peak = jnp.max(scores, axis=1, keepdims=True)
        weights = jnp.exp(scores - own_peak)
        own_total = jnp.sum(weights, axis=1, keepdims=True)
        own_acc = jnp.dot(
            weights.astype(jnp.bfloat16), pkv_ref[1, :, kv_columns], preferred_element_type=jnp.float32
        )
        first_peak = peak_ref[:, head : head + 1]
        peak = jnp.maximum(first_peak, own_peak)
        first_scale = jnp.exp(first_peak - peak)
        own_scale = jnp.exp(own_peak - peak)
        total = total_ref[:, head : head + 1] * first_scale + own_total * own_scale
        summed = acc_ref[:, columns] * first_scale + own_acc * own_scale
        out_ref[:, columns] = (summed / total).astype(out_ref.dtype)


def whole(shape):
    return pl.BlockSpec(shape, lambda: (0,) * len(shape))


def attend_local(queries, prefix_key_values, suffix_key_values, request_ids):
    local_count, model_width = queries.shape
    column, row = request_ids.reshape(local_count, 1), request_ids.reshape(1, local_count)
    inputs = (column, row, queries, prefix_key_values, suffix_key_values)
    stats = jax.ShapeDtypeStruct((local_count, QUERY_HEADS), jnp.float32)
    return pl.pallas_call(
        local_kernel,
        in_specs=[whole(x.shape) for x in inputs],
        out_specs=[whole((local_count, model_width)), whole(stats.shape), whole(stats.shape)],
        out_shape=[jax.ShapeDtypeStruct((local_count, model_width), jnp.float32), stats, stats],
        compiler_params=pltpu.CompilerParams(vmem_limit_bytes=48 * 1024 * 1024),
    )(*inputs)


def attend_merge(queries, prefix_key_values, acc, peak, total):
    inputs = (queries, prefix_key_values, acc, peak, total)
    return pl.pallas_call(
        merge_kernel,
        in_specs=[whole(x.shape) for x in inputs],
        out_specs=whole(queries.shape),
        out_shape=jax.ShapeDtypeStruct(queries.shape, jnp.bfloat16),
        compiler_params=pltpu.CompilerParams(vmem_limit_bytes=48 * 1024 * 1024),
    )(*inputs)


def expert_kernel(rows_ref, gate_ref, up_ref, down_ref, out_ref, acc_ref):
    step = pl.program_id(0)

    @pl.when(step == 0)
    def _():
        acc_ref[...] = jnp.zeros_like(acc_ref)

    rows = rows_ref[...]
    gated = jnp.dot(rows, gate_ref[...], preferred_element_type=jnp.float32)
    lifted = jnp.dot(rows, up_ref[...], preferred_element_type=jnp.float32)
    active = (jnp.maximum(gated, 0.0) * lifted).astype(jnp.bfloat16)
    acc_ref[...] += jnp.dot(active, down_ref[...], preferred_element_type=jnp.float32)

    @pl.when(step == pl.num_programs(0) - 1)
    def _():
        out_ref[...] = acc_ref[...].astype(out_ref.dtype)


def expert_ffn(rows, gate_experts, up_experts, down_experts):
    count, width = rows.shape
    hidden = gate_experts.shape[2]
    block = 256 if hidden % 256 == 0 else hidden
    return pl.pallas_call(
        expert_kernel,
        grid=(hidden // block,),
        in_specs=[
            pl.BlockSpec((count, width), lambda f: (0, 0)),
            pl.BlockSpec((None, width, block), lambda f: (0, 0, f)),
            pl.BlockSpec((None, width, block), lambda f: (0, 0, f)),
            pl.BlockSpec((None, block, width), lambda f: (0, f, 0)),
        ],
        out_specs=pl.BlockSpec((count, width), lambda f: (0, 0)),
        out_shape=jax.ShapeDtypeStruct((count, width), jnp.bfloat16),
        scratch_shapes=[pltpu.VMEM((count, width), jnp.float32)],
        compiler_params=pltpu.CompilerParams(vmem_limit_bytes=48 * 1024 * 1024),
    )(rows, gate_experts, up_experts, down_experts)


def on_device(
    residual,
    queries,
    suffix_key_values,
    prefix_key_values,
    request_ids,
    out_weight,
    norm_gain,
    expert_routes,
    route_gates,
    gate_experts,
    up_experts,
    down_experts,
):
    local_count = queries.shape[0]
    model_width = queries.shape[1]
    chip_count = lax.axis_size("chip")
    req_count = lax.axis_size("req")
    by_req = lax.all_to_all(
        jnp.broadcast_to(prefix_key_values[:, None], (2, req_count) + prefix_key_values.shape[1:]),
        "req",
        split_axis=1,
        concat_axis=1,
        tiled=True,
    ).reshape(2, req_count * prefix_key_values.shape[1], prefix_key_values.shape[2])
    spread = jnp.broadcast_to(by_req[:, None], (2, chip_count) + by_req.shape[1:])
    by_chip = lax.all_to_all(spread, "chip", split_axis=1, concat_axis=1, tiled=True).reshape(
        2, chip_count * by_req.shape[1], by_req.shape[2]
    )
    partner_half = lax.ppermute(by_chip, "core", [(0, 1), (1, 0)])
    acc, peak, total = attend_local(queries, by_chip, suffix_key_values, request_ids)
    attended = attend_merge(queries, partner_half, acc, peak, total)
    section = attended
    projected = jnp.dot(
        section,
        lax.all_gather(out_weight, "req", axis=0, tiled=True),
        preferred_element_type=jnp.float32,
    )
    stream = residual.astype(jnp.float32) + projected
    inverse_rms = lax.rsqrt(jnp.mean(stream * stream, axis=1, keepdims=True) + EPSILON)
    normed = (stream * inverse_rms * norm_gain[None, :]).astype(jnp.bfloat16)
    top_count = expert_routes.shape[1]
    expert_count = gate_experts.shape[0] * lax.axis_size(EXP)
    capacity = 3 * top_count * local_count // (2 * expert_count)
    flat_routes = expert_routes.reshape(-1)
    matches = (flat_routes[:, None] == jnp.arange(expert_count, dtype=jnp.int32)[None, :]).astype(
        jnp.int32
    )
    route_count = flat_routes.shape[0]
    earlier = (
        lax.broadcasted_iota(jnp.int32, (route_count, route_count), 0)
        > lax.broadcasted_iota(jnp.int32, (route_count, route_count), 1)
    ).astype(jnp.bfloat16)
    before = jnp.dot(earlier, matches.astype(jnp.bfloat16), preferred_element_type=jnp.float32)
    slot_rank = jnp.sum(before.astype(jnp.int32) * matches, axis=1)
    slot_of_route = flat_routes * capacity + slot_rank
    slot_ids = jnp.arange(expert_count * capacity, dtype=jnp.int32)
    hit = slot_of_route.reshape(local_count, top_count)[:, :, None] == slot_ids[None, None, :]
    dispatch = jnp.any(hit, axis=1).astype(jnp.bfloat16)
    outgoing = (
        jnp.einsum("ts,tf->sf", dispatch, normed, preferred_element_type=jnp.float32)
        .astype(jnp.bfloat16)
        .reshape(expert_count, capacity, model_width)
    )
    slot_rows = lax.all_to_all(outgoing, EXP, split_axis=0, concat_axis=0, tiled=True)
    senders, slot_count, features = slot_rows.shape
    flat_rows = slot_rows.reshape(senders * slot_count, features)
    produced = expert_ffn(flat_rows, gate_experts, up_experts, down_experts)
    computed = produced.reshape(senders, slot_count, features)
    returned = lax.all_to_all(computed, EXP, split_axis=0, concat_axis=0, tiled=True)
    slot_gates = jnp.sum(jnp.where(hit, route_gates[:, :, None], 0.0), axis=1)
    combined = jnp.dot(
        slot_gates,
        returned.reshape(expert_count * capacity, model_width).astype(jnp.float32),
        precision=lax.Precision.HIGHEST,
        preferred_element_type=jnp.float32,
    )
    return (stream + combined).astype(jnp.bfloat16)


def solution(mesh):
    placed = (
        P(("req", "chip", "core"), None),
        P(("req", "chip", "core"), None),
        P(None, ("req", "chip", "core"), None),
        P(None, ("req", "chip", "core"), None),
        P(("req", "chip", "core"), None),
        P("req", None),
        P(),
        P(("req", "chip", "core"), None),
        P(("req", "chip", "core"), None),
        P(EXP, None, None),
        P(EXP, None, None),
        P(EXP, None, None),
    )
    req_count, exp_count = mesh.devices.shape
    split_mesh = Mesh(
        mesh.devices.reshape(req_count, exp_count // 2, 2), ("req", "chip", "core")
    )
    return jax.shard_map(
        on_device, mesh=split_mesh, in_specs=placed, out_specs=P(("req", "chip", "core"), None), check_vma=False
    )
```

```python
import math

import jax
import jax.numpy as jnp
from jax import lax
from jax.sharding import Mesh, PartitionSpec as P
from jax.experimental import pallas as pl
from jax.experimental.pallas import tpu as pltpu

QUERY_HEADS = 12
KEY_VALUE_HEADS = 2
HEAD_SIZE = 128


EPSILON = 1e-06
MASKED_SCORE = -1e30
EXP = ("chip", "core")


def head_scores(q_ref, keys, head):
    columns = slice(head * HEAD_SIZE, (head + 1) * HEAD_SIZE)
    contract = (((1,), (1,)), ((), ()))
    return lax.dot_general(
        q_ref[:, columns], keys, contract, preferred_element_type=jnp.float32
    ) * (1.0 / math.sqrt(HEAD_SIZE))


def local_kernel(rid_col_ref, rid_row_ref, q_ref, pkv_ref, skv_ref, acc_ref, peak_ref, total_ref):
    local_count = q_ref.shape[0]
    position = lax.broadcasted_iota(jnp.int32, (local_count, local_count), 0)
    key_position = lax.broadcasted_iota(jnp.int32, (local_count, local_count), 1)
    allowed = (rid_col_ref[...] == rid_row_ref[...]) & (position >= key_position)
    for head in range(QUERY_HEADS // KEY_VALUE_HEADS):
        columns = slice(head * HEAD_SIZE, (head + 1) * HEAD_SIZE)
        prefix_scores = head_scores(q_ref, pkv_ref[0], head)
        suffix_scores = head_scores(q_ref, skv_ref[0], head)
        suffix_scores = jnp.where(allowed, suffix_scores, MASKED_SCORE)
        peak = jnp.maximum(
            jnp.max(prefix_scores, axis=1, keepdims=True),
            jnp.max(suffix_scores, axis=1, keepdims=True),
        )
        prefix_weights = jnp.exp(prefix_scores - peak)
        suffix_weights = jnp.where(allowed, jnp.exp(suffix_scores - peak), 0.0)
        total_ref[:, head : head + 1] = jnp.sum(prefix_weights, axis=1, keepdims=True) + jnp.sum(
            suffix_weights, axis=1, keepdims=True
        )
        peak_ref[:, head : head + 1] = peak
        acc_ref[:, columns] = jnp.dot(
            prefix_weights.astype(jnp.bfloat16), pkv_ref[1], preferred_element_type=jnp.float32
        ) + jnp.dot(
            suffix_weights.astype(jnp.bfloat16), skv_ref[1], preferred_element_type=jnp.float32
        )


def merge_kernel(q_ref, pkv_ref, acc_ref, peak_ref, total_ref, out_ref):
    for head in range(QUERY_HEADS // KEY_VALUE_HEADS):
        columns = slice(head * HEAD_SIZE, (head + 1) * HEAD_SIZE)
        scores = head_scores(q_ref, pkv_ref[0], head)
        own_peak = jnp.max(scores, axis=1, keepdims=True)
        weights = jnp.exp(scores - own_peak)
        own_total = jnp.sum(weights, axis=1, keepdims=True)
        own_acc = jnp.dot(
            weights.astype(jnp.bfloat16), pkv_ref[1], preferred_element_type=jnp.float32
        )
        first_peak = peak_ref[:, head : head + 1]
        peak = jnp.maximum(first_peak, own_peak)
        first_scale = jnp.exp(first_peak - peak)
        own_scale = jnp.exp(own_peak - peak)
        total = total_ref[:, head : head + 1] * first_scale + own_total * own_scale
        summed = acc_ref[:, columns] * first_scale + own_acc * own_scale
        out_ref[:, columns] = (summed / total).astype(out_ref.dtype)


def group_specs(local_count, model_width, prefix_count):
    group_width = model_width // KEY_VALUE_HEADS
    groups = QUERY_HEADS // KEY_VALUE_HEADS
    rows = pl.BlockSpec((local_count, group_width), lambda g: (0, g))
    keys = pl.BlockSpec((2, prefix_count, HEAD_SIZE), lambda g: (0, 0, g))
    stats = pl.BlockSpec((None, local_count, groups), lambda g: (g, 0, 0))
    return rows, keys, stats


def attend_local(queries, prefix_key_values, suffix_key_values, request_ids):
    local_count, model_width = queries.shape
    rows, keys, stats = group_specs(local_count, model_width, prefix_key_values.shape[1])
    stat_shape = jax.ShapeDtypeStruct(
        (KEY_VALUE_HEADS, local_count, QUERY_HEADS // KEY_VALUE_HEADS), jnp.float32
    )
    return pl.pallas_call(
        local_kernel,
        grid=(KEY_VALUE_HEADS,),
        in_specs=[
            pl.BlockSpec((local_count, 1), lambda g: (0, 0)),
            pl.BlockSpec((1, local_count), lambda g: (0, 0)),
            rows,
            keys,
            pl.BlockSpec((2, local_count, HEAD_SIZE), lambda g: (0, 0, g)),
        ],
        out_specs=[rows, stats, stats],
        out_shape=[
            jax.ShapeDtypeStruct((local_count, model_width), jnp.float32),
            stat_shape,
            stat_shape,
        ],
        compiler_params=pltpu.CompilerParams(vmem_limit_bytes=48 * 1024 * 1024),
    )(request_ids.reshape(local_count, 1), request_ids.reshape(1, local_count), queries,
      prefix_key_values, suffix_key_values)


def attend_merge(queries, prefix_key_values, acc, peak, total):
    local_count, model_width = queries.shape
    rows, keys, stats = group_specs(local_count, model_width, prefix_key_values.shape[1])
    return pl.pallas_call(
        merge_kernel,
        grid=(KEY_VALUE_HEADS,),
        in_specs=[rows, keys, rows, stats, stats],
        out_specs=rows,
        out_shape=jax.ShapeDtypeStruct(queries.shape, jnp.bfloat16),
        compiler_params=pltpu.CompilerParams(vmem_limit_bytes=48 * 1024 * 1024),
    )(queries, prefix_key_values, acc, peak, total)


def expert_kernel(rows_ref, gate_ref, up_ref, down_ref, out_ref, acc_ref):
    step = pl.program_id(0)

    @pl.when(step == 0)
    def _():
        acc_ref[...] = jnp.zeros_like(acc_ref)

    rows = rows_ref[...]
    gated = jnp.dot(rows, gate_ref[...], preferred_element_type=jnp.float32)
    lifted = jnp.dot(rows, up_ref[...], preferred_element_type=jnp.float32)
    active = (jnp.maximum(gated, 0.0) * lifted).astype(jnp.bfloat16)
    acc_ref[...] += jnp.dot(active, down_ref[...], preferred_element_type=jnp.float32)

    @pl.when(step == pl.num_programs(0) - 1)
    def _():
        out_ref[...] = acc_ref[...].astype(out_ref.dtype)


def expert_ffn(rows, gate_experts, up_experts, down_experts):
    count, width = rows.shape
    hidden = gate_experts.shape[2]
    block = 256 if hidden % 256 == 0 else hidden
    return pl.pallas_call(
        expert_kernel,
        grid=(hidden // block,),
        in_specs=[
            pl.BlockSpec((count, width), lambda f: (0, 0)),
            pl.BlockSpec((None, width, block), lambda f: (0, 0, f)),
            pl.BlockSpec((None, width, block), lambda f: (0, 0, f)),
            pl.BlockSpec((None, block, width), lambda f: (0, f, 0)),
        ],
        out_specs=pl.BlockSpec((count, width), lambda f: (0, 0)),
        out_shape=jax.ShapeDtypeStruct((count, width), jnp.bfloat16),
        scratch_shapes=[pltpu.VMEM((count, width), jnp.float32)],
        compiler_params=pltpu.CompilerParams(vmem_limit_bytes=48 * 1024 * 1024),
    )(rows, gate_experts, up_experts, down_experts)


def on_device(
    residual,
    queries,
    suffix_key_values,
    prefix_key_values,
    request_ids,
    out_weight,
    norm_gain,
    expert_routes,
    route_gates,
    gate_experts,
    up_experts,
    down_experts,
):
    local_count = queries.shape[0]
    model_width = queries.shape[1]
    chip_count = lax.axis_size("chip")
    req_count = lax.axis_size("req")
    by_req = lax.all_to_all(
        jnp.broadcast_to(prefix_key_values[:, None], (2, req_count) + prefix_key_values.shape[1:]),
        "req",
        split_axis=1,
        concat_axis=1,
        tiled=True,
    ).reshape(2, req_count * prefix_key_values.shape[1], prefix_key_values.shape[2])
    spread = jnp.broadcast_to(by_req[:, None], (2, chip_count) + by_req.shape[1:])
    by_chip = lax.all_to_all(spread, "chip", split_axis=1, concat_axis=1, tiled=True).reshape(
        2, chip_count * by_req.shape[1], by_req.shape[2]
    )
    partner_half = lax.ppermute(by_chip, "core", [(0, 1), (1, 0)])
    acc, peak, total = attend_local(queries, by_chip, suffix_key_values, request_ids)
    attended = attend_merge(queries, partner_half, acc, peak, total)
    section = attended
    projected = jnp.dot(
        section,
        lax.all_gather(out_weight, "req", axis=0, tiled=True),
        preferred_element_type=jnp.float32,
    )
    stream = residual.astype(jnp.float32) + projected
    inverse_rms = lax.rsqrt(jnp.mean(stream * stream, axis=1, keepdims=True) + EPSILON)
    normed = (stream * inverse_rms * norm_gain[None, :]).astype(jnp.bfloat16)
    top_count = expert_routes.shape[1]
    expert_count = gate_experts.shape[0] * lax.axis_size(EXP)
    capacity = 3 * top_count * local_count // (2 * expert_count)
    flat_routes = expert_routes.reshape(-1)
    matches = (flat_routes[:, None] == jnp.arange(expert_count, dtype=jnp.int32)[None, :]).astype(
        jnp.int32
    )
    route_count = flat_routes.shape[0]
    earlier = (
        lax.broadcasted_iota(jnp.int32, (route_count, route_count), 0)
        > lax.broadcasted_iota(jnp.int32, (route_count, route_count), 1)
    ).astype(jnp.bfloat16)
    before = jnp.dot(earlier, matches.astype(jnp.bfloat16), preferred_element_type=jnp.float32)
    slot_rank = jnp.sum(before.astype(jnp.int32) * matches, axis=1)
    slot_of_route = flat_routes * capacity + slot_rank
    slot_ids = jnp.arange(expert_count * capacity, dtype=jnp.int32)
    hit = slot_of_route.reshape(local_count, top_count)[:, :, None] == slot_ids[None, None, :]
    dispatch = jnp.any(hit, axis=1).astype(jnp.bfloat16)
    outgoing = (
        jnp.einsum("ts,tf->sf", dispatch, normed, preferred_element_type=jnp.float32)
        .astype(jnp.bfloat16)
        .reshape(expert_count, capacity, model_width)
    )
    slot_rows = lax.all_to_all(outgoing, EXP, split_axis=0, concat_axis=0, tiled=True)
    senders, slot_count, features = slot_rows.shape
    flat_rows = slot_rows.reshape(senders * slot_count, features)
    produced = expert_ffn(flat_rows, gate_experts, up_experts, down_experts)
    computed = produced.reshape(senders, slot_count, features)
    returned = lax.all_to_all(computed, EXP, split_axis=0, concat_axis=0, tiled=True)
    slot_gates = jnp.sum(jnp.where(hit, route_gates[:, :, None], 0.0), axis=1)
    combined = jnp.dot(
        slot_gates,
        returned.reshape(expert_count * capacity, model_width).astype(jnp.float32),
        precision=lax.Precision.HIGHEST,
        preferred_element_type=jnp.float32,
    )
    return (stream + combined).astype(jnp.bfloat16)


def solution(mesh):
    placed = (
        P(("req", "chip", "core"), None),
        P(("req", "chip", "core"), None),
        P(None, ("req", "chip", "core"), None),
        P(None, ("req", "chip", "core"), None),
        P(("req", "chip", "core"), None),
        P("req", None),
        P(),
        P(("req", "chip", "core"), None),
        P(("req", "chip", "core"), None),
        P(EXP, None, None),
        P(EXP, None, None),
        P(EXP, None, None),
    )
    req_count, exp_count = mesh.devices.shape
    split_mesh = Mesh(
        mesh.devices.reshape(req_count, exp_count // 2, 2), ("req", "chip", "core")
    )
    return jax.shard_map(
        on_device, mesh=split_mesh, in_specs=placed, out_specs=P(("req", "chip", "core"), None), check_vma=False
    )
```

```python
import math

import jax
import jax.numpy as jnp
from jax import lax
from jax.sharding import Mesh, PartitionSpec as P
from jax.experimental import pallas as pl
from jax.experimental.pallas import tpu as pltpu

QUERY_HEADS = 12
KEY_VALUE_HEADS = 2
HEAD_SIZE = 128


EPSILON = 1e-06
MASKED_SCORE = -1e30
EXP = ("chip", "core")


def head_scores(q_ref, keys, head):
    columns = slice(head * HEAD_SIZE, (head + 1) * HEAD_SIZE)
    contract = (((1,), (1,)), ((), ()))
    return lax.dot_general(
        q_ref[:, columns], keys, contract, preferred_element_type=jnp.float32
    ) * (1.0 / math.sqrt(HEAD_SIZE))


def local_kernel(rid_col_ref, rid_row_ref, q_ref, pkv_ref, skv_ref, acc_ref, peak_ref, total_ref):
    local_count = q_ref.shape[0]
    position = lax.broadcasted_iota(jnp.int32, (local_count, local_count), 0)
    key_position = lax.broadcasted_iota(jnp.int32, (local_count, local_count), 1)
    allowed = (rid_col_ref[...] == rid_row_ref[...]) & (position >= key_position)
    groups = QUERY_HEADS // KEY_VALUE_HEADS
    for head in range(QUERY_HEADS):
        kv_columns = slice((head // groups) * HEAD_SIZE, (head // groups + 1) * HEAD_SIZE)
        columns = slice(head * HEAD_SIZE, (head + 1) * HEAD_SIZE)
        prefix_scores = head_scores(q_ref, pkv_ref[0, :, kv_columns], head)
        suffix_scores = head_scores(q_ref, skv_ref[0, :, kv_columns], head)
        suffix_scores = jnp.where(allowed, suffix_scores, MASKED_SCORE)
        peak = jnp.maximum(
            jnp.max(prefix_scores, axis=1, keepdims=True),
            jnp.max(suffix_scores, axis=1, keepdims=True),
        )
        prefix_weights = jnp.exp(prefix_scores - peak)
        suffix_weights = jnp.where(allowed, jnp.exp(suffix_scores - peak), 0.0)
        total_ref[:, head : head + 1] = jnp.sum(prefix_weights, axis=1, keepdims=True) + jnp.sum(
            suffix_weights, axis=1, keepdims=True
        )
        peak_ref[:, head : head + 1] = peak
        acc_ref[:, columns] = jnp.dot(
            prefix_weights.astype(jnp.bfloat16),
            pkv_ref[1, :, kv_columns],
            preferred_element_type=jnp.float32,
        ) + jnp.dot(
            suffix_weights.astype(jnp.bfloat16),
            skv_ref[1, :, kv_columns],
            preferred_element_type=jnp.float32,
        )


def merge_kernel(q_ref, pkv_ref, acc_ref, peak_ref, total_ref, out_ref):
    groups = QUERY_HEADS // KEY_VALUE_HEADS
    for head in range(QUERY_HEADS):
        kv_columns = slice((head // groups) * HEAD_SIZE, (head // groups + 1) * HEAD_SIZE)
        columns = slice(head * HEAD_SIZE, (head + 1) * HEAD_SIZE)
        scores = head_scores(q_ref, pkv_ref[0, :, kv_columns], head)
        own_peak = jnp.max(scores, axis=1, keepdims=True)
        weights = jnp.exp(scores - own_peak)
        own_total = jnp.sum(weights, axis=1, keepdims=True)
        own_acc = jnp.dot(
            weights.astype(jnp.bfloat16), pkv_ref[1, :, kv_columns], preferred_element_type=jnp.float32
        )
        first_peak = peak_ref[:, head : head + 1]
        peak = jnp.maximum(first_peak, own_peak)
        first_scale = jnp.exp(first_peak - peak)
        own_scale = jnp.exp(own_peak - peak)
        total = total_ref[:, head : head + 1] * first_scale + own_total * own_scale
        summed = acc_ref[:, columns] * first_scale + own_acc * own_scale
        out_ref[:, columns] = (summed / total).astype(out_ref.dtype)


def whole(shape):
    return pl.BlockSpec(shape, lambda: (0,) * len(shape))


def attend_local(queries, prefix_key_values, suffix_key_values, request_ids):
    local_count, model_width = queries.shape
    column, row = request_ids.reshape(local_count, 1), request_ids.reshape(1, local_count)
    inputs = (column, row, queries, prefix_key_values, suffix_key_values)
    stats = jax.ShapeDtypeStruct((local_count, QUERY_HEADS), jnp.float32)
    return pl.pallas_call(
        local_kernel,
        in_specs=[whole(x.shape) for x in inputs],
        out_specs=[whole((local_count, model_width)), whole(stats.shape), whole(stats.shape)],
        out_shape=[jax.ShapeDtypeStruct((local_count, model_width), jnp.float32), stats, stats],
        compiler_params=pltpu.CompilerParams(vmem_limit_bytes=48 * 1024 * 1024),
    )(*inputs)


def attend_merge(queries, prefix_key_values, acc, peak, total):
    inputs = (queries, prefix_key_values, acc, peak, total)
    return pl.pallas_call(
        merge_kernel,
        in_specs=[whole(x.shape) for x in inputs],
        out_specs=whole(queries.shape),
        out_shape=jax.ShapeDtypeStruct(queries.shape, jnp.bfloat16),
        compiler_params=pltpu.CompilerParams(vmem_limit_bytes=48 * 1024 * 1024),
    )(*inputs)


def expert_kernel(rows_ref, gate_ref, up_ref, down_ref, out_ref, acc_ref):
    step = pl.program_id(0)

    @pl.when(step == 0)
    def _():
        acc_ref[...] = jnp.zeros_like(acc_ref)

    rows = rows_ref[...]
    gated = jnp.dot(rows, gate_ref[...], preferred_element_type=jnp.float32)
    lifted = jnp.dot(rows, up_ref[...], preferred_element_type=jnp.float32)
    active = (jnp.maximum(gated, 0.0) * lifted).astype(jnp.bfloat16)
    acc_ref[...] += jnp.dot(active, down_ref[...], preferred_element_type=jnp.float32)

    @pl.when(step == pl.num_programs(0) - 1)
    def _():
        out_ref[...] = acc_ref[...].astype(out_ref.dtype)


def expert_ffn(rows, gate_experts, up_experts, down_experts):
    count, width = rows.shape
    hidden = gate_experts.shape[2]
    block = 256 if hidden % 256 == 0 else hidden
    return pl.pallas_call(
        expert_kernel,
        grid=(hidden // block,),
        in_specs=[
            pl.BlockSpec((count, width), lambda f: (0, 0)),
            pl.BlockSpec((None, width, block), lambda f: (0, 0, f)),
            pl.BlockSpec((None, width, block), lambda f: (0, 0, f)),
            pl.BlockSpec((None, block, width), lambda f: (0, f, 0)),
        ],
        out_specs=pl.BlockSpec((count, width), lambda f: (0, 0)),
        out_shape=jax.ShapeDtypeStruct((count, width), jnp.bfloat16),
        scratch_shapes=[pltpu.VMEM((count, width), jnp.float32)],
        compiler_params=pltpu.CompilerParams(vmem_limit_bytes=48 * 1024 * 1024),
    )(rows, gate_experts, up_experts, down_experts)


def on_device(
    residual,
    queries,
    suffix_key_values,
    prefix_key_values,
    request_ids,
    out_weight,
    norm_gain,
    expert_routes,
    route_gates,
    gate_experts,
    up_experts,
    down_experts,
):
    local_count = queries.shape[0]
    model_width = queries.shape[1]
    chip_count = lax.axis_size("chip")
    req_count = lax.axis_size("req")
    by_req = lax.all_to_all(
        jnp.broadcast_to(prefix_key_values[:, None], (2, req_count) + prefix_key_values.shape[1:]),
        "req",
        split_axis=1,
        concat_axis=1,
        tiled=True,
    ).reshape(2, req_count * prefix_key_values.shape[1], prefix_key_values.shape[2])
    spread = jnp.broadcast_to(by_req[:, None], (2, chip_count) + by_req.shape[1:])
    by_chip = lax.all_to_all(spread, "chip", split_axis=1, concat_axis=1, tiled=True).reshape(
        2, chip_count * by_req.shape[1], by_req.shape[2]
    )
    partner_half = lax.ppermute(by_chip, "core", [(0, 1), (1, 0)])
    acc, peak, total = attend_local(queries, by_chip, suffix_key_values, request_ids)
    attended = attend_merge(queries, partner_half, acc, peak, total)
    section = attended
    projected = jnp.dot(
        section,
        lax.all_gather(out_weight, "req", axis=0, tiled=True),
        preferred_element_type=jnp.float32,
    )
    stream = residual.astype(jnp.float32) + projected
    inverse_rms = lax.rsqrt(jnp.mean(stream * stream, axis=1, keepdims=True) + EPSILON)
    normed = (stream * inverse_rms * norm_gain[None, :]).astype(jnp.bfloat16)
    top_count = expert_routes.shape[1]
    expert_count = gate_experts.shape[0] * lax.axis_size(EXP)
    capacity = 3 * top_count * local_count // (2 * expert_count)
    flat_routes = expert_routes.reshape(-1)
    matches = (flat_routes[:, None] == jnp.arange(expert_count, dtype=jnp.int32)[None, :]).astype(
        jnp.int32
    )
    route_count = flat_routes.shape[0]
    earlier = (
        lax.broadcasted_iota(jnp.int32, (route_count, route_count), 0)
        > lax.broadcasted_iota(jnp.int32, (route_count, route_count), 1)
    ).astype(jnp.bfloat16)
    before = jnp.dot(earlier, matches.astype(jnp.bfloat16), preferred_element_type=jnp.float32)
    slot_rank = jnp.sum(before.astype(jnp.int32) * matches, axis=1)
    slot_of_route = flat_routes * capacity + slot_rank
    slot_ids = jnp.arange(expert_count * capacity, dtype=jnp.int32)
    hit = slot_of_route.reshape(local_count, top_count)[:, :, None] == slot_ids[None, None, :]
    dispatch = jnp.any(hit, axis=1).astype(jnp.bfloat16)
    outgoing = (
        jnp.einsum("ts,tf->sf", dispatch, normed, preferred_element_type=jnp.float32)
        .astype(jnp.bfloat16)
        .reshape(expert_count, capacity, model_width)
    )
    slot_rows = lax.all_to_all(outgoing, EXP, split_axis=0, concat_axis=0, tiled=True)
    senders, slot_count, features = slot_rows.shape
    flat_rows = slot_rows.reshape(senders * slot_count, features)
    produced = expert_ffn(flat_rows, gate_experts, up_experts, down_experts)
    computed = produced.reshape(senders, slot_count, features)
    returned = lax.all_to_all(computed, EXP, split_axis=0, concat_axis=0, tiled=True)
    slot_gates = jnp.sum(jnp.where(hit, route_gates[:, :, None], 0.0), axis=1)
    returned_rows = returned.reshape(expert_count * capacity, model_width)
    combined = jnp.zeros((local_count, model_width), jnp.float32)
    remainder = slot_gates
    for _ in range(3):
        piece = remainder.astype(jnp.bfloat16)
        combined = combined + jnp.dot(piece, returned_rows, preferred_element_type=jnp.float32)
        remainder = remainder - piece.astype(jnp.float32)
    return (stream + combined).astype(jnp.bfloat16)


def solution(mesh):
    placed = (
        P(("req", "chip", "core"), None),
        P(("req", "chip", "core"), None),
        P(None, ("req", "chip", "core"), None),
        P(None, ("req", "chip", "core"), None),
        P(("req", "chip", "core"), None),
        P("req", None),
        P(),
        P(("req", "chip", "core"), None),
        P(("req", "chip", "core"), None),
        P(EXP, None, None),
        P(EXP, None, None),
        P(EXP, None, None),
    )
    req_count, exp_count = mesh.devices.shape
    split_mesh = Mesh(
        mesh.devices.reshape(req_count, exp_count // 2, 2), ("req", "chip", "core")
    )
    return jax.shard_map(
        on_device, mesh=split_mesh, in_specs=placed, out_specs=P(("req", "chip", "core"), None), check_vma=False
    )
```

```python
import math

import jax
import jax.numpy as jnp
from jax import lax
from jax.sharding import Mesh, PartitionSpec as P
from jax.experimental import pallas as pl
from jax.experimental.pallas import tpu as pltpu

QUERY_HEADS = 12
KEY_VALUE_HEADS = 2
HEAD_SIZE = 128


EPSILON = 1e-06
MASKED_SCORE = -1e30
EXP = ("chip", "core")


def head_scores(q_ref, keys, head):
    columns = slice(head * HEAD_SIZE, (head + 1) * HEAD_SIZE)
    contract = (((1,), (1,)), ((), ()))
    return lax.dot_general(
        q_ref[:, columns], keys, contract, preferred_element_type=jnp.float32
    ) * (1.0 / math.sqrt(HEAD_SIZE))


def local_kernel(rid_col_ref, rid_row_ref, q_ref, pkv_ref, skv_ref, acc_ref, peak_ref, total_ref):
    local_count = q_ref.shape[0]
    position = lax.broadcasted_iota(jnp.int32, (local_count, local_count), 0)
    key_position = lax.broadcasted_iota(jnp.int32, (local_count, local_count), 1)
    allowed = (rid_col_ref[...] == rid_row_ref[...]) & (position >= key_position)
    groups = QUERY_HEADS // KEY_VALUE_HEADS
    for head in range(QUERY_HEADS):
        kv_columns = slice((head // groups) * HEAD_SIZE, (head // groups + 1) * HEAD_SIZE)
        columns = slice(head * HEAD_SIZE, (head + 1) * HEAD_SIZE)
        prefix_scores = head_scores(q_ref, pkv_ref[0, :, kv_columns], head)
        suffix_scores = head_scores(q_ref, skv_ref[0, :, kv_columns], head)
        suffix_scores = jnp.where(allowed, suffix_scores, MASKED_SCORE)
        peak = jnp.maximum(
            jnp.max(prefix_scores, axis=1, keepdims=True),
            jnp.max(suffix_scores, axis=1, keepdims=True),
        )
        prefix_weights = jnp.exp(prefix_scores - peak)
        suffix_weights = jnp.where(allowed, jnp.exp(suffix_scores - peak), 0.0)
        total_ref[:, head : head + 1] = jnp.sum(prefix_weights, axis=1, keepdims=True) + jnp.sum(
            suffix_weights, axis=1, keepdims=True
        )
        peak_ref[:, head : head + 1] = peak
        acc_ref[:, columns] = jnp.dot(
            prefix_weights.astype(jnp.bfloat16),
            pkv_ref[1, :, kv_columns],
            preferred_element_type=jnp.float32,
        ) + jnp.dot(
            suffix_weights.astype(jnp.bfloat16),
            skv_ref[1, :, kv_columns],
            preferred_element_type=jnp.float32,
        )


def merge_kernel(q_ref, pkv_ref, acc_ref, peak_ref, total_ref, out_ref):
    groups = QUERY_HEADS // KEY_VALUE_HEADS
    for head in range(QUERY_HEADS):
        kv_columns = slice((head // groups) * HEAD_SIZE, (head // groups + 1) * HEAD_SIZE)
        columns = slice(head * HEAD_SIZE, (head + 1) * HEAD_SIZE)
        scores = head_scores(q_ref, pkv_ref[0, :, kv_columns], head)
        own_peak = jnp.max(scores, axis=1, keepdims=True)
        weights = jnp.exp(scores - own_peak)
        own_total = jnp.sum(weights, axis=1, keepdims=True)
        own_acc = jnp.dot(
            weights.astype(jnp.bfloat16), pkv_ref[1, :, kv_columns], preferred_element_type=jnp.float32
        )
        first_peak = peak_ref[:, head : head + 1]
        peak = jnp.maximum(first_peak, own_peak)
        first_scale = jnp.exp(first_peak - peak)
        own_scale = jnp.exp(own_peak - peak)
        total = total_ref[:, head : head + 1] * first_scale + own_total * own_scale
        summed = acc_ref[:, columns] * first_scale + own_acc * own_scale
        out_ref[:, columns] = (summed / total).astype(out_ref.dtype)


def whole(shape):
    return pl.BlockSpec(shape, lambda: (0,) * len(shape))


def attend_local(queries, prefix_key_values, suffix_key_values, request_ids):
    local_count, model_width = queries.shape
    column, row = request_ids.reshape(local_count, 1), request_ids.reshape(1, local_count)
    inputs = (column, row, queries, prefix_key_values, suffix_key_values)
    stats = jax.ShapeDtypeStruct((local_count, QUERY_HEADS), jnp.float32)
    return pl.pallas_call(
        local_kernel,
        in_specs=[whole(x.shape) for x in inputs],
        out_specs=[whole((local_count, model_width)), whole(stats.shape), whole(stats.shape)],
        out_shape=[jax.ShapeDtypeStruct((local_count, model_width), jnp.float32), stats, stats],
        compiler_params=pltpu.CompilerParams(vmem_limit_bytes=48 * 1024 * 1024),
    )(*inputs)


def attend_merge(queries, prefix_key_values, acc, peak, total):
    inputs = (queries, prefix_key_values, acc, peak, total)
    return pl.pallas_call(
        merge_kernel,
        in_specs=[whole(x.shape) for x in inputs],
        out_specs=whole(queries.shape),
        out_shape=jax.ShapeDtypeStruct(queries.shape, jnp.bfloat16),
        compiler_params=pltpu.CompilerParams(vmem_limit_bytes=48 * 1024 * 1024),
    )(*inputs)


def expert_kernel(rows_ref, gate_ref, up_ref, down_ref, out_ref, acc_ref):
    step = pl.program_id(0)

    @pl.when(step == 0)
    def _():
        acc_ref[...] = jnp.zeros_like(acc_ref)

    rows = rows_ref[...]
    gated = jnp.dot(rows, gate_ref[...], preferred_element_type=jnp.float32)
    lifted = jnp.dot(rows, up_ref[...], preferred_element_type=jnp.float32)
    active = (jnp.maximum(gated, 0.0) * lifted).astype(jnp.bfloat16)
    acc_ref[...] += jnp.dot(active, down_ref[...], preferred_element_type=jnp.float32)

    @pl.when(step == pl.num_programs(0) - 1)
    def _():
        out_ref[...] = acc_ref[...].astype(out_ref.dtype)


def expert_ffn(rows, gate_experts, up_experts, down_experts):
    count, width = rows.shape
    hidden = gate_experts.shape[2]
    block = 128 if hidden % 128 == 0 else hidden
    return pl.pallas_call(
        expert_kernel,
        grid=(hidden // block,),
        in_specs=[
            pl.BlockSpec((count, width), lambda f: (0, 0)),
            pl.BlockSpec((None, width, block), lambda f: (0, 0, f)),
            pl.BlockSpec((None, width, block), lambda f: (0, 0, f)),
            pl.BlockSpec((None, block, width), lambda f: (0, f, 0)),
        ],
        out_specs=pl.BlockSpec((count, width), lambda f: (0, 0)),
        out_shape=jax.ShapeDtypeStruct((count, width), jnp.bfloat16),
        scratch_shapes=[pltpu.VMEM((count, width), jnp.float32)],
        compiler_params=pltpu.CompilerParams(vmem_limit_bytes=48 * 1024 * 1024),
    )(rows, gate_experts, up_experts, down_experts)


def on_device(
    residual,
    queries,
    suffix_key_values,
    prefix_key_values,
    request_ids,
    out_weight,
    norm_gain,
    expert_routes,
    route_gates,
    gate_experts,
    up_experts,
    down_experts,
):
    local_count = queries.shape[0]
    model_width = queries.shape[1]
    chip_count = lax.axis_size("chip")
    req_count = lax.axis_size("req")
    by_req = lax.all_to_all(
        jnp.broadcast_to(prefix_key_values[:, None], (2, req_count) + prefix_key_values.shape[1:]),
        "req",
        split_axis=1,
        concat_axis=1,
        tiled=True,
    ).reshape(2, req_count * prefix_key_values.shape[1], prefix_key_values.shape[2])
    spread = jnp.broadcast_to(by_req[:, None], (2, chip_count) + by_req.shape[1:])
    by_chip = lax.all_to_all(spread, "chip", split_axis=1, concat_axis=1, tiled=True).reshape(
        2, chip_count * by_req.shape[1], by_req.shape[2]
    )
    partner_half = lax.ppermute(by_chip, "core", [(0, 1), (1, 0)])
    acc, peak, total = attend_local(queries, by_chip, suffix_key_values, request_ids)
    attended = attend_merge(queries, partner_half, acc, peak, total)
    section = attended
    projected = jnp.dot(
        section,
        lax.all_gather(out_weight, "req", axis=0, tiled=True),
        preferred_element_type=jnp.float32,
    )
    stream = residual.astype(jnp.float32) + projected
    inverse_rms = lax.rsqrt(jnp.mean(stream * stream, axis=1, keepdims=True) + EPSILON)
    normed = (stream * inverse_rms * norm_gain[None, :]).astype(jnp.bfloat16)
    top_count = expert_routes.shape[1]
    expert_count = gate_experts.shape[0] * lax.axis_size(EXP)
    capacity = 3 * top_count * local_count // (2 * expert_count)
    flat_routes = expert_routes.reshape(-1)
    matches = (flat_routes[:, None] == jnp.arange(expert_count, dtype=jnp.int32)[None, :]).astype(
        jnp.int32
    )
    route_count = flat_routes.shape[0]
    earlier = (
        lax.broadcasted_iota(jnp.int32, (route_count, route_count), 0)
        > lax.broadcasted_iota(jnp.int32, (route_count, route_count), 1)
    ).astype(jnp.bfloat16)
    before = jnp.dot(earlier, matches.astype(jnp.bfloat16), preferred_element_type=jnp.float32)
    slot_rank = jnp.sum(before.astype(jnp.int32) * matches, axis=1)
    slot_of_route = flat_routes * capacity + slot_rank
    slot_ids = jnp.arange(expert_count * capacity, dtype=jnp.int32)
    hit = slot_of_route.reshape(local_count, top_count)[:, :, None] == slot_ids[None, None, :]
    dispatch = jnp.any(hit, axis=1).astype(jnp.bfloat16)
    outgoing = (
        jnp.einsum("ts,tf->sf", dispatch, normed, preferred_element_type=jnp.float32)
        .astype(jnp.bfloat16)
        .reshape(expert_count, capacity, model_width)
    )
    slot_rows = lax.all_to_all(outgoing, EXP, split_axis=0, concat_axis=0, tiled=True)
    senders, slot_count, features = slot_rows.shape
    flat_rows = slot_rows.reshape(senders * slot_count, features)
    produced = expert_ffn(flat_rows, gate_experts, up_experts, down_experts)
    computed = produced.reshape(senders, slot_count, features)
    returned = lax.all_to_all(computed, EXP, split_axis=0, concat_axis=0, tiled=True)
    slot_gates = jnp.sum(jnp.where(hit, route_gates[:, :, None], 0.0), axis=1)
    combined = jnp.dot(
        slot_gates,
        returned.reshape(expert_count * capacity, model_width).astype(jnp.float32),
        precision=lax.Precision.HIGHEST,
        preferred_element_type=jnp.float32,
    )
    return (stream + combined).astype(jnp.bfloat16)


def solution(mesh):
    placed = (
        P(("req", "chip", "core"), None),
        P(("req", "chip", "core"), None),
        P(None, ("req", "chip", "core"), None),
        P(None, ("req", "chip", "core"), None),
        P(("req", "chip", "core"), None),
        P("req", None),
        P(),
        P(("req", "chip", "core"), None),
        P(("req", "chip", "core"), None),
        P(EXP, None, None),
        P(EXP, None, None),
        P(EXP, None, None),
    )
    req_count, exp_count = mesh.devices.shape
    split_mesh = Mesh(
        mesh.devices.reshape(req_count, exp_count // 2, 2), ("req", "chip", "core")
    )
    return jax.shard_map(
        on_device, mesh=split_mesh, in_specs=placed, out_specs=P(("req", "chip", "core"), None), check_vma=False
    )
```

```python
import math

import jax
import jax.numpy as jnp
from jax import lax
from jax.sharding import Mesh, PartitionSpec as P
from jax.experimental import pallas as pl
from jax.experimental.pallas import tpu as pltpu

QUERY_HEADS = 12
KEY_VALUE_HEADS = 2
HEAD_SIZE = 128


EPSILON = 1e-06
MASKED_SCORE = -1e30
EXP = ("chip", "core")


def head_scores(q_ref, keys, head):
    columns = slice(head * HEAD_SIZE, (head + 1) * HEAD_SIZE)
    contract = (((1,), (1,)), ((), ()))
    return lax.dot_general(
        q_ref[:, columns], keys, contract, preferred_element_type=jnp.float32
    ) * (1.0 / math.sqrt(HEAD_SIZE))


def local_kernel(rid_col_ref, rid_row_ref, q_ref, pkv_ref, skv_ref, acc_ref, peak_ref, total_ref):
    local_count = q_ref.shape[0]
    position = lax.broadcasted_iota(jnp.int32, (local_count, local_count), 0)
    key_position = lax.broadcasted_iota(jnp.int32, (local_count, local_count), 1)
    allowed = (rid_col_ref[...] == rid_row_ref[...]) & (position >= key_position)
    groups = QUERY_HEADS // KEY_VALUE_HEADS
    for head in range(QUERY_HEADS):
        kv_columns = slice((head // groups) * HEAD_SIZE, (head // groups + 1) * HEAD_SIZE)
        columns = slice(head * HEAD_SIZE, (head + 1) * HEAD_SIZE)
        prefix_scores = head_scores(q_ref, pkv_ref[0, :, kv_columns], head)
        suffix_scores = head_scores(q_ref, skv_ref[0, :, kv_columns], head)
        suffix_scores = jnp.where(allowed, suffix_scores, MASKED_SCORE)
        peak = jnp.maximum(
            jnp.max(prefix_scores, axis=1, keepdims=True),
            jnp.max(suffix_scores, axis=1, keepdims=True),
        )
        prefix_weights = jnp.exp(prefix_scores - peak)
        suffix_weights = jnp.where(allowed, jnp.exp(suffix_scores - peak), 0.0)
        total_ref[:, head : head + 1] = jnp.sum(prefix_weights, axis=1, keepdims=True) + jnp.sum(
            suffix_weights, axis=1, keepdims=True
        )
        peak_ref[:, head : head + 1] = peak
        acc_ref[:, columns] = jnp.dot(
            prefix_weights.astype(jnp.bfloat16),
            pkv_ref[1, :, kv_columns],
            preferred_element_type=jnp.float32,
        ) + jnp.dot(
            suffix_weights.astype(jnp.bfloat16),
            skv_ref[1, :, kv_columns],
            preferred_element_type=jnp.float32,
        )


def merge_kernel(q_ref, pkv_ref, acc_ref, peak_ref, total_ref, out_ref):
    groups = QUERY_HEADS // KEY_VALUE_HEADS
    for head in range(QUERY_HEADS):
        kv_columns = slice((head // groups) * HEAD_SIZE, (head // groups + 1) * HEAD_SIZE)
        columns = slice(head * HEAD_SIZE, (head + 1) * HEAD_SIZE)
        scores = head_scores(q_ref, pkv_ref[0, :, kv_columns], head)
        own_peak = jnp.max(scores, axis=1, keepdims=True)
        weights = jnp.exp(scores - own_peak)
        own_total = jnp.sum(weights, axis=1, keepdims=True)
        own_acc = jnp.dot(
            weights.astype(jnp.bfloat16), pkv_ref[1, :, kv_columns], preferred_element_type=jnp.float32
        )
        first_peak = peak_ref[:, head : head + 1]
        peak = jnp.maximum(first_peak, own_peak)
        first_scale = jnp.exp(first_peak - peak)
        own_scale = jnp.exp(own_peak - peak)
        total = total_ref[:, head : head + 1] * first_scale + own_total * own_scale
        summed = acc_ref[:, columns] * first_scale + own_acc * own_scale
        out_ref[:, columns] = (summed / total).astype(out_ref.dtype)


def whole(shape):
    return pl.BlockSpec(shape, lambda: (0,) * len(shape))


def attend_local(queries, prefix_key_values, suffix_key_values, request_ids):
    local_count, model_width = queries.shape
    column, row = request_ids.reshape(local_count, 1), request_ids.reshape(1, local_count)
    inputs = (column, row, queries, prefix_key_values, suffix_key_values)
    stats = jax.ShapeDtypeStruct((local_count, QUERY_HEADS), jnp.float32)
    return pl.pallas_call(
        local_kernel,
        in_specs=[whole(x.shape) for x in inputs],
        out_specs=[whole((local_count, model_width)), whole(stats.shape), whole(stats.shape)],
        out_shape=[jax.ShapeDtypeStruct((local_count, model_width), jnp.float32), stats, stats],
        compiler_params=pltpu.CompilerParams(vmem_limit_bytes=48 * 1024 * 1024),
    )(*inputs)


def attend_merge(queries, prefix_key_values, acc, peak, total):
    inputs = (queries, prefix_key_values, acc, peak, total)
    return pl.pallas_call(
        merge_kernel,
        in_specs=[whole(x.shape) for x in inputs],
        out_specs=whole(queries.shape),
        out_shape=jax.ShapeDtypeStruct(queries.shape, jnp.bfloat16),
        compiler_params=pltpu.CompilerParams(vmem_limit_bytes=48 * 1024 * 1024),
    )(*inputs)


def expert_kernel(rows_ref, gate_ref, up_ref, down_ref, out_ref, acc_ref):
    step = pl.program_id(0)
    first = step == 0
    last = step == pl.num_programs(0) - 1
    rows = rows_ref[...]
    gated = jnp.dot(rows, gate_ref[...], preferred_element_type=jnp.float32)
    lifted = jnp.dot(rows, up_ref[...], preferred_element_type=jnp.float32)
    active = (jnp.maximum(gated, 0.0) * lifted).astype(jnp.bfloat16)
    part = jnp.dot(active, down_ref[...], preferred_element_type=jnp.float32)

    @pl.when(first & jnp.logical_not(last))
    def _():
        acc_ref[...] = part

    @pl.when(jnp.logical_not(first) & jnp.logical_not(last))
    def _():
        acc_ref[...] += part

    @pl.when(last & jnp.logical_not(first))
    def _():
        out_ref[...] = (acc_ref[...] + part).astype(out_ref.dtype)

    @pl.when(first & last)
    def _():
        out_ref[...] = part.astype(out_ref.dtype)


def expert_ffn(rows, gate_experts, up_experts, down_experts):
    count, width = rows.shape
    hidden = gate_experts.shape[2]
    block = 256 if hidden % 256 == 0 else hidden
    return pl.pallas_call(
        expert_kernel,
        grid=(hidden // block,),
        in_specs=[
            pl.BlockSpec((count, width), lambda f: (0, 0)),
            pl.BlockSpec((None, width, block), lambda f: (0, 0, f)),
            pl.BlockSpec((None, width, block), lambda f: (0, 0, f)),
            pl.BlockSpec((None, block, width), lambda f: (0, f, 0)),
        ],
        out_specs=pl.BlockSpec((count, width), lambda f: (0, 0)),
        out_shape=jax.ShapeDtypeStruct((count, width), jnp.bfloat16),
        scratch_shapes=[pltpu.VMEM((count, width), jnp.float32)],
        compiler_params=pltpu.CompilerParams(vmem_limit_bytes=48 * 1024 * 1024),
    )(rows, gate_experts, up_experts, down_experts)


def on_device(
    residual,
    queries,
    suffix_key_values,
    prefix_key_values,
    request_ids,
    out_weight,
    norm_gain,
    expert_routes,
    route_gates,
    gate_experts,
    up_experts,
    down_experts,
):
    local_count = queries.shape[0]
    model_width = queries.shape[1]
    chip_count = lax.axis_size("chip")
    req_count = lax.axis_size("req")
    by_req = lax.all_to_all(
        jnp.broadcast_to(prefix_key_values[:, None], (2, req_count) + prefix_key_values.shape[1:]),
        "req",
        split_axis=1,
        concat_axis=1,
        tiled=True,
    ).reshape(2, req_count * prefix_key_values.shape[1], prefix_key_values.shape[2])
    spread = jnp.broadcast_to(by_req[:, None], (2, chip_count) + by_req.shape[1:])
    by_chip = lax.all_to_all(spread, "chip", split_axis=1, concat_axis=1, tiled=True).reshape(
        2, chip_count * by_req.shape[1], by_req.shape[2]
    )
    partner_half = lax.ppermute(by_chip, "core", [(0, 1), (1, 0)])
    acc, peak, total = attend_local(queries, by_chip, suffix_key_values, request_ids)
    attended = attend_merge(queries, partner_half, acc, peak, total)
    section = attended
    projected = jnp.dot(
        section,
        lax.all_gather(out_weight, "req", axis=0, tiled=True),
        preferred_element_type=jnp.float32,
    )
    stream = residual.astype(jnp.float32) + projected
    inverse_rms = lax.rsqrt(jnp.mean(stream * stream, axis=1, keepdims=True) + EPSILON)
    normed = (stream * inverse_rms * norm_gain[None, :]).astype(jnp.bfloat16)
    top_count = expert_routes.shape[1]
    expert_count = gate_experts.shape[0] * lax.axis_size(EXP)
    capacity = 3 * top_count * local_count // (2 * expert_count)
    flat_routes = expert_routes.reshape(-1)
    matches = (flat_routes[:, None] == jnp.arange(expert_count, dtype=jnp.int32)[None, :]).astype(
        jnp.int32
    )
    route_count = flat_routes.shape[0]
    earlier = (
        lax.broadcasted_iota(jnp.int32, (route_count, route_count), 0)
        > lax.broadcasted_iota(jnp.int32, (route_count, route_count), 1)
    ).astype(jnp.bfloat16)
    before = jnp.dot(earlier, matches.astype(jnp.bfloat16), preferred_element_type=jnp.float32)
    slot_rank = jnp.sum(before.astype(jnp.int32) * matches, axis=1)
    slot_of_route = flat_routes * capacity + slot_rank
    slot_ids = jnp.arange(expert_count * capacity, dtype=jnp.int32)
    hit = slot_of_route.reshape(local_count, top_count)[:, :, None] == slot_ids[None, None, :]
    dispatch = jnp.any(hit, axis=1).astype(jnp.bfloat16)
    outgoing = (
        jnp.einsum("ts,tf->sf", dispatch, normed, preferred_element_type=jnp.float32)
        .astype(jnp.bfloat16)
        .reshape(expert_count, capacity, model_width)
    )
    slot_rows = lax.all_to_all(outgoing, EXP, split_axis=0, concat_axis=0, tiled=True)
    senders, slot_count, features = slot_rows.shape
    flat_rows = slot_rows.reshape(senders * slot_count, features)
    produced = expert_ffn(flat_rows, gate_experts, up_experts, down_experts)
    computed = produced.reshape(senders, slot_count, features)
    returned = lax.all_to_all(computed, EXP, split_axis=0, concat_axis=0, tiled=True)
    slot_gates = jnp.sum(jnp.where(hit, route_gates[:, :, None], 0.0), axis=1)
    combined = jnp.dot(
        slot_gates,
        returned.reshape(expert_count * capacity, model_width).astype(jnp.float32),
        precision=lax.Precision.HIGHEST,
        preferred_element_type=jnp.float32,
    )
    return (stream + combined).astype(jnp.bfloat16)


def solution(mesh):
    placed = (
        P(("req", "chip", "core"), None),
        P(("req", "chip", "core"), None),
        P(None, ("req", "chip", "core"), None),
        P(None, ("req", "chip", "core"), None),
        P(("req", "chip", "core"), None),
        P("req", None),
        P(),
        P(("req", "chip", "core"), None),
        P(("req", "chip", "core"), None),
        P(EXP, None, None),
        P(EXP, None, None),
        P(EXP, None, None),
    )
    req_count, exp_count = mesh.devices.shape
    split_mesh = Mesh(
        mesh.devices.reshape(req_count, exp_count // 2, 2), ("req", "chip", "core")
    )
    return jax.shard_map(
        on_device, mesh=split_mesh, in_specs=placed, out_specs=P(("req", "chip", "core"), None), check_vma=False
    )
```

```python
import math

import jax
import jax.numpy as jnp
from jax import lax
from jax.sharding import Mesh, PartitionSpec as P
from jax.experimental import pallas as pl
from jax.experimental.pallas import tpu as pltpu

QUERY_HEADS = 12
KEY_VALUE_HEADS = 2
HEAD_SIZE = 128


EPSILON = 1e-06
MASKED_SCORE = -1e30
EXP = ("chip", "core")


def head_scores(q_ref, keys, head):
    columns = slice(head * HEAD_SIZE, (head + 1) * HEAD_SIZE)
    contract = (((1,), (1,)), ((), ()))
    return lax.dot_general(
        q_ref[:, columns], keys, contract, preferred_element_type=jnp.float32
    ) * (1.0 / math.sqrt(HEAD_SIZE))


def local_kernel(rid_col_ref, rid_row_ref, q_ref, pkv_ref, skv_ref, acc_ref, peak_ref, total_ref):
    local_count = q_ref.shape[0]
    position = lax.broadcasted_iota(jnp.int32, (local_count, local_count), 0)
    key_position = lax.broadcasted_iota(jnp.int32, (local_count, local_count), 1)
    allowed = (rid_col_ref[...] == rid_row_ref[...]) & (position >= key_position)
    groups = QUERY_HEADS // KEY_VALUE_HEADS
    for head in range(QUERY_HEADS):
        kv_columns = slice((head // groups) * HEAD_SIZE, (head // groups + 1) * HEAD_SIZE)
        columns = slice(head * HEAD_SIZE, (head + 1) * HEAD_SIZE)
        prefix_scores = head_scores(q_ref, pkv_ref[0, :, kv_columns], head)
        suffix_scores = head_scores(q_ref, skv_ref[0, :, kv_columns], head)
        suffix_scores = jnp.where(allowed, suffix_scores, MASKED_SCORE)
        peak = jnp.maximum(
            jnp.max(prefix_scores, axis=1, keepdims=True),
            jnp.max(suffix_scores, axis=1, keepdims=True),
        )
        prefix_weights = jnp.exp(prefix_scores - peak)
        suffix_weights = jnp.where(allowed, jnp.exp(suffix_scores - peak), 0.0)
        total_ref[:, head : head + 1] = jnp.sum(prefix_weights, axis=1, keepdims=True) + jnp.sum(
            suffix_weights, axis=1, keepdims=True
        )
        peak_ref[:, head : head + 1] = peak
        acc_ref[:, columns] = jnp.dot(
            prefix_weights.astype(jnp.bfloat16),
            pkv_ref[1, :, kv_columns],
            preferred_element_type=jnp.float32,
        ) + jnp.dot(
            suffix_weights.astype(jnp.bfloat16),
            skv_ref[1, :, kv_columns],
            preferred_element_type=jnp.float32,
        )


def merge_kernel(q_ref, pkv_ref, acc_ref, peak_ref, total_ref, out_ref):
    groups = QUERY_HEADS // KEY_VALUE_HEADS
    for head in range(QUERY_HEADS):
        kv_columns = slice((head // groups) * HEAD_SIZE, (head // groups + 1) * HEAD_SIZE)
        columns = slice(head * HEAD_SIZE, (head + 1) * HEAD_SIZE)
        scores = head_scores(q_ref, pkv_ref[0, :, kv_columns], head)
        own_peak = jnp.max(scores, axis=1, keepdims=True)
        weights = jnp.exp(scores - own_peak)
        own_total = jnp.sum(weights, axis=1, keepdims=True)
        own_acc = jnp.dot(
            weights.astype(jnp.bfloat16), pkv_ref[1, :, kv_columns], preferred_element_type=jnp.float32
        )
        first_peak = peak_ref[:, head : head + 1]
        peak = jnp.maximum(first_peak, own_peak)
        first_scale = jnp.exp(first_peak - peak)
        own_scale = jnp.exp(own_peak - peak)
        total = total_ref[:, head : head + 1] * first_scale + own_total * own_scale
        summed = acc_ref[:, columns] * first_scale + own_acc * own_scale
        out_ref[:, columns] = (summed * (1.0 / total)).astype(out_ref.dtype)


def whole(shape):
    return pl.BlockSpec(shape, lambda: (0,) * len(shape))


def attend_local(queries, prefix_key_values, suffix_key_values, request_ids):
    local_count, model_width = queries.shape
    column, row = request_ids.reshape(local_count, 1), request_ids.reshape(1, local_count)
    inputs = (column, row, queries, prefix_key_values, suffix_key_values)
    stats = jax.ShapeDtypeStruct((local_count, QUERY_HEADS), jnp.float32)
    return pl.pallas_call(
        local_kernel,
        in_specs=[whole(x.shape) for x in inputs],
        out_specs=[whole((local_count, model_width)), whole(stats.shape), whole(stats.shape)],
        out_shape=[jax.ShapeDtypeStruct((local_count, model_width), jnp.float32), stats, stats],
        compiler_params=pltpu.CompilerParams(vmem_limit_bytes=48 * 1024 * 1024),
    )(*inputs)


def attend_merge(queries, prefix_key_values, acc, peak, total):
    inputs = (queries, prefix_key_values, acc, peak, total)
    return pl.pallas_call(
        merge_kernel,
        in_specs=[whole(x.shape) for x in inputs],
        out_specs=whole(queries.shape),
        out_shape=jax.ShapeDtypeStruct(queries.shape, jnp.bfloat16),
        compiler_params=pltpu.CompilerParams(vmem_limit_bytes=48 * 1024 * 1024),
    )(*inputs)


def expert_kernel(rows_ref, gate_ref, up_ref, down_ref, out_ref, acc_ref):
    step = pl.program_id(0)

    @pl.when(step == 0)
    def _():
        acc_ref[...] = jnp.zeros_like(acc_ref)

    rows = rows_ref[...]
    gated = jnp.dot(rows, gate_ref[...], preferred_element_type=jnp.float32)
    lifted = jnp.dot(rows, up_ref[...], preferred_element_type=jnp.float32)
    active = (jnp.maximum(gated, 0.0) * lifted).astype(jnp.bfloat16)
    acc_ref[...] += jnp.dot(active, down_ref[...], preferred_element_type=jnp.float32)

    @pl.when(step == pl.num_programs(0) - 1)
    def _():
        out_ref[...] = acc_ref[...].astype(out_ref.dtype)


def expert_ffn(rows, gate_experts, up_experts, down_experts):
    count, width = rows.shape
    hidden = gate_experts.shape[2]
    block = 256 if hidden % 256 == 0 else hidden
    return pl.pallas_call(
        expert_kernel,
        grid=(hidden // block,),
        in_specs=[
            pl.BlockSpec((count, width), lambda f: (0, 0)),
            pl.BlockSpec((None, width, block), lambda f: (0, 0, f)),
            pl.BlockSpec((None, width, block), lambda f: (0, 0, f)),
            pl.BlockSpec((None, block, width), lambda f: (0, f, 0)),
        ],
        out_specs=pl.BlockSpec((count, width), lambda f: (0, 0)),
        out_shape=jax.ShapeDtypeStruct((count, width), jnp.bfloat16),
        scratch_shapes=[pltpu.VMEM((count, width), jnp.float32)],
        compiler_params=pltpu.CompilerParams(vmem_limit_bytes=48 * 1024 * 1024),
    )(rows, gate_experts, up_experts, down_experts)


def on_device(
    residual,
    queries,
    suffix_key_values,
    prefix_key_values,
    request_ids,
    out_weight,
    norm_gain,
    expert_routes,
    route_gates,
    gate_experts,
    up_experts,
    down_experts,
):
    local_count = queries.shape[0]
    model_width = queries.shape[1]
    chip_count = lax.axis_size("chip")
    req_count = lax.axis_size("req")
    by_req = lax.all_to_all(
        jnp.broadcast_to(prefix_key_values[:, None], (2, req_count) + prefix_key_values.shape[1:]),
        "req",
        split_axis=1,
        concat_axis=1,
        tiled=True,
    ).reshape(2, req_count * prefix_key_values.shape[1], prefix_key_values.shape[2])
    spread = jnp.broadcast_to(by_req[:, None], (2, chip_count) + by_req.shape[1:])
    by_chip = lax.all_to_all(spread, "chip", split_axis=1, concat_axis=1, tiled=True).reshape(
        2, chip_count * by_req.shape[1], by_req.shape[2]
    )
    partner_half = lax.ppermute(by_chip, "core", [(0, 1), (1, 0)])
    acc, peak, total = attend_local(queries, by_chip, suffix_key_values, request_ids)
    attended = attend_merge(queries, partner_half, acc, peak, total)
    section = attended
    projected = jnp.dot(
        section,
        lax.all_gather(out_weight, "req", axis=0, tiled=True),
        preferred_element_type=jnp.float32,
    )
    stream = residual.astype(jnp.float32) + projected
    inverse_rms = lax.rsqrt(jnp.mean(stream * stream, axis=1, keepdims=True) + EPSILON)
    normed = (stream * inverse_rms * norm_gain[None, :]).astype(jnp.bfloat16)
    top_count = expert_routes.shape[1]
    expert_count = gate_experts.shape[0] * lax.axis_size(EXP)
    capacity = 3 * top_count * local_count // (2 * expert_count)
    flat_routes = expert_routes.reshape(-1)
    matches = (flat_routes[:, None] == jnp.arange(expert_count, dtype=jnp.int32)[None, :]).astype(
        jnp.int32
    )
    route_count = flat_routes.shape[0]
    earlier = (
        lax.broadcasted_iota(jnp.int32, (route_count, route_count), 0)
        > lax.broadcasted_iota(jnp.int32, (route_count, route_count), 1)
    ).astype(jnp.bfloat16)
    before = jnp.dot(earlier, matches.astype(jnp.bfloat16), preferred_element_type=jnp.float32)
    slot_rank = jnp.sum(before.astype(jnp.int32) * matches, axis=1)
    slot_of_route = flat_routes * capacity + slot_rank
    slot_ids = jnp.arange(expert_count * capacity, dtype=jnp.int32)
    hit = slot_of_route.reshape(local_count, top_count)[:, :, None] == slot_ids[None, None, :]
    dispatch = jnp.any(hit, axis=1).astype(jnp.bfloat16)
    outgoing = (
        jnp.einsum("ts,tf->sf", dispatch, normed, preferred_element_type=jnp.float32)
        .astype(jnp.bfloat16)
        .reshape(expert_count, capacity, model_width)
    )
    slot_rows = lax.all_to_all(outgoing, EXP, split_axis=0, concat_axis=0, tiled=True)
    senders, slot_count, features = slot_rows.shape
    flat_rows = slot_rows.reshape(senders * slot_count, features)
    produced = expert_ffn(flat_rows, gate_experts, up_experts, down_experts)
    computed = produced.reshape(senders, slot_count, features)
    returned = lax.all_to_all(computed, EXP, split_axis=0, concat_axis=0, tiled=True)
    slot_gates = jnp.sum(jnp.where(hit, route_gates[:, :, None], 0.0), axis=1)
    combined = jnp.dot(
        slot_gates,
        returned.reshape(expert_count * capacity, model_width).astype(jnp.float32),
        precision=lax.Precision.HIGHEST,
        preferred_element_type=jnp.float32,
    )
    return (stream + combined).astype(jnp.bfloat16)


def solution(mesh):
    placed = (
        P(("req", "chip", "core"), None),
        P(("req", "chip", "core"), None),
        P(None, ("req", "chip", "core"), None),
        P(None, ("req", "chip", "core"), None),
        P(("req", "chip", "core"), None),
        P("req", None),
        P(),
        P(("req", "chip", "core"), None),
        P(("req", "chip", "core"), None),
        P(EXP, None, None),
        P(EXP, None, None),
        P(EXP, None, None),
    )
    req_count, exp_count = mesh.devices.shape
    split_mesh = Mesh(
        mesh.devices.reshape(req_count, exp_count // 2, 2), ("req", "chip", "core")
    )
    return jax.shard_map(
        on_device, mesh=split_mesh, in_specs=placed, out_specs=P(("req", "chip", "core"), None), check_vma=False
    )
```

```python
import math

import jax
import jax.numpy as jnp
from jax import lax
from jax.sharding import Mesh, PartitionSpec as P
from jax.experimental import pallas as pl
from jax.experimental.pallas import tpu as pltpu

QUERY_HEADS = 12
KEY_VALUE_HEADS = 2
HEAD_SIZE = 128


EPSILON = 1e-06
MASKED_SCORE = -1e30
EXP = ("chip", "core")


def head_scores(q_ref, keys, head):
    columns = slice(head * HEAD_SIZE, (head + 1) * HEAD_SIZE)
    contract = (((1,), (1,)), ((), ()))
    return lax.dot_general(
        q_ref[:, columns], keys, contract, preferred_element_type=jnp.float32
    ) * (1.0 / math.sqrt(HEAD_SIZE))


def local_kernel(rid_col_ref, rid_row_ref, q_ref, pkv_ref, skv_ref, acc_ref, peak_ref, total_ref):
    local_count = q_ref.shape[0]
    position = lax.broadcasted_iota(jnp.int32, (local_count, local_count), 0)
    key_position = lax.broadcasted_iota(jnp.int32, (local_count, local_count), 1)
    allowed = (rid_col_ref[...] == rid_row_ref[...]) & (position >= key_position)
    groups = QUERY_HEADS // KEY_VALUE_HEADS
    for head in range(QUERY_HEADS):
        kv_columns = slice((head // groups) * HEAD_SIZE, (head // groups + 1) * HEAD_SIZE)
        columns = slice(head * HEAD_SIZE, (head + 1) * HEAD_SIZE)
        prefix_scores = head_scores(q_ref, pkv_ref[0, :, kv_columns], head)
        suffix_scores = head_scores(q_ref, skv_ref[0, :, kv_columns], head)
        suffix_scores = jnp.where(allowed, suffix_scores, MASKED_SCORE)
        peak = jnp.maximum(
            jnp.max(prefix_scores, axis=1, keepdims=True),
            jnp.max(suffix_scores, axis=1, keepdims=True),
        )
        prefix_weights = jnp.exp(prefix_scores - peak)
        suffix_weights = jnp.where(allowed, jnp.exp(suffix_scores - peak), 0.0)
        total_ref[:, head : head + 1] = jnp.sum(prefix_weights, axis=1, keepdims=True) + jnp.sum(
            suffix_weights, axis=1, keepdims=True
        )
        peak_ref[:, head : head + 1] = peak
        acc_ref[:, columns] = jnp.dot(
            prefix_weights.astype(jnp.bfloat16),
            pkv_ref[1, :, kv_columns],
            preferred_element_type=jnp.float32,
        ) + jnp.dot(
            suffix_weights.astype(jnp.bfloat16),
            skv_ref[1, :, kv_columns],
            preferred_element_type=jnp.float32,
        )


def merge_kernel(q_ref, pkv_ref, acc_ref, peak_ref, total_ref, out_ref):
    groups = QUERY_HEADS // KEY_VALUE_HEADS
    for head in range(QUERY_HEADS):
        kv_columns = slice((head // groups) * HEAD_SIZE, (head // groups + 1) * HEAD_SIZE)
        columns = slice(head * HEAD_SIZE, (head + 1) * HEAD_SIZE)
        scores = head_scores(q_ref, pkv_ref[0, :, kv_columns], head)
        own_peak = jnp.max(scores, axis=1, keepdims=True)
        weights = jnp.exp(scores - own_peak)
        own_total = jnp.sum(weights, axis=1, keepdims=True)
        own_acc = jnp.dot(
            weights.astype(jnp.bfloat16), pkv_ref[1, :, kv_columns], preferred_element_type=jnp.float32
        )
        first_peak = peak_ref[:, head : head + 1]
        peak = jnp.maximum(first_peak, own_peak)
        first_scale = jnp.exp(first_peak - peak)
        own_scale = jnp.exp(own_peak - peak)
        total = total_ref[:, head : head + 1] * first_scale + own_total * own_scale
        summed = acc_ref[:, columns] * first_scale + own_acc * own_scale
        out_ref[:, columns] = (summed / total).astype(out_ref.dtype)


def whole(shape):
    return pl.BlockSpec(shape, lambda: (0,) * len(shape))


def attend_local(queries, prefix_key_values, suffix_key_values, request_ids):
    local_count, model_width = queries.shape
    column, row = request_ids.reshape(local_count, 1), request_ids.reshape(1, local_count)
    inputs = (column, row, queries, prefix_key_values, suffix_key_values)
    stats = jax.ShapeDtypeStruct((local_count, QUERY_HEADS), jnp.float32)
    return pl.pallas_call(
        local_kernel,
        in_specs=[whole(x.shape) for x in inputs],
        out_specs=[whole((local_count, model_width)), whole(stats.shape), whole(stats.shape)],
        out_shape=[jax.ShapeDtypeStruct((local_count, model_width), jnp.float32), stats, stats],
        compiler_params=pltpu.CompilerParams(vmem_limit_bytes=48 * 1024 * 1024),
    )(*inputs)


def attend_merge(queries, prefix_key_values, acc, peak, total):
    inputs = (queries, prefix_key_values, acc, peak, total)
    return pl.pallas_call(
        merge_kernel,
        in_specs=[whole(x.shape) for x in inputs],
        out_specs=whole(queries.shape),
        out_shape=jax.ShapeDtypeStruct(queries.shape, jnp.bfloat16),
        compiler_params=pltpu.CompilerParams(vmem_limit_bytes=48 * 1024 * 1024),
    )(*inputs)


def expert_kernel(rows_ref, gate_ref, up_ref, down_ref, out_ref, acc_ref):
    step = pl.program_id(0)

    @pl.when(step == 0)
    def _():
        acc_ref[...] = jnp.zeros_like(acc_ref)

    rows = rows_ref[...]
    gated = jnp.dot(rows, gate_ref[...], preferred_element_type=jnp.float32)
    lifted = jnp.dot(rows, up_ref[...], preferred_element_type=jnp.float32)
    active = (jnp.maximum(gated, 0.0) * lifted).astype(jnp.bfloat16)
    acc_ref[...] += jnp.dot(active, down_ref[...], preferred_element_type=jnp.float32)

    @pl.when(step == pl.num_programs(0) - 1)
    def _():
        out_ref[...] = acc_ref[...].astype(out_ref.dtype)


def expert_ffn(rows, gate_experts, up_experts, down_experts):
    count, width = rows.shape
    hidden = gate_experts.shape[2]
    block = 384 if hidden % 384 == 0 else hidden
    return pl.pallas_call(
        expert_kernel,
        grid=(hidden // block,),
        in_specs=[
            pl.BlockSpec((count, width), lambda f: (0, 0)),
            pl.BlockSpec((None, width, block), lambda f: (0, 0, f)),
            pl.BlockSpec((None, width, block), lambda f: (0, 0, f)),
            pl.BlockSpec((None, block, width), lambda f: (0, f, 0)),
        ],
        out_specs=pl.BlockSpec((count, width), lambda f: (0, 0)),
        out_shape=jax.ShapeDtypeStruct((count, width), jnp.bfloat16),
        scratch_shapes=[pltpu.VMEM((count, width), jnp.float32)],
        compiler_params=pltpu.CompilerParams(vmem_limit_bytes=48 * 1024 * 1024),
    )(rows, gate_experts, up_experts, down_experts)


def on_device(
    residual,
    queries,
    suffix_key_values,
    prefix_key_values,
    request_ids,
    out_weight,
    norm_gain,
    expert_routes,
    route_gates,
    gate_experts,
    up_experts,
    down_experts,
):
    local_count = queries.shape[0]
    model_width = queries.shape[1]
    chip_count = lax.axis_size("chip")
    req_count = lax.axis_size("req")
    by_req = lax.all_to_all(
        jnp.broadcast_to(prefix_key_values[:, None], (2, req_count) + prefix_key_values.shape[1:]),
        "req",
        split_axis=1,
        concat_axis=1,
        tiled=True,
    ).reshape(2, req_count * prefix_key_values.shape[1], prefix_key_values.shape[2])
    spread = jnp.broadcast_to(by_req[:, None], (2, chip_count) + by_req.shape[1:])
    by_chip = lax.all_to_all(spread, "chip", split_axis=1, concat_axis=1, tiled=True).reshape(
        2, chip_count * by_req.shape[1], by_req.shape[2]
    )
    partner_half = lax.ppermute(by_chip, "core", [(0, 1), (1, 0)])
    acc, peak, total = attend_local(queries, by_chip, suffix_key_values, request_ids)
    attended = attend_merge(queries, partner_half, acc, peak, total)
    section = attended
    projected = jnp.dot(
        section,
        lax.all_gather(out_weight, "req", axis=0, tiled=True),
        preferred_element_type=jnp.float32,
    )
    stream = residual.astype(jnp.float32) + projected
    inverse_rms = lax.rsqrt(jnp.mean(stream * stream, axis=1, keepdims=True) + EPSILON)
    normed = (stream * inverse_rms * norm_gain[None, :]).astype(jnp.bfloat16)
    top_count = expert_routes.shape[1]
    expert_count = gate_experts.shape[0] * lax.axis_size(EXP)
    capacity = 3 * top_count * local_count // (2 * expert_count)
    flat_routes = expert_routes.reshape(-1)
    matches = (flat_routes[:, None] == jnp.arange(expert_count, dtype=jnp.int32)[None, :]).astype(
        jnp.int32
    )
    route_count = flat_routes.shape[0]
    earlier = (
        lax.broadcasted_iota(jnp.int32, (route_count, route_count), 0)
        > lax.broadcasted_iota(jnp.int32, (route_count, route_count), 1)
    ).astype(jnp.bfloat16)
    before = jnp.dot(earlier, matches.astype(jnp.bfloat16), preferred_element_type=jnp.float32)
    slot_rank = jnp.sum(before.astype(jnp.int32) * matches, axis=1)
    slot_of_route = flat_routes * capacity + slot_rank
    slot_ids = jnp.arange(expert_count * capacity, dtype=jnp.int32)
    hit = slot_of_route.reshape(local_count, top_count)[:, :, None] == slot_ids[None, None, :]
    dispatch = jnp.any(hit, axis=1).astype(jnp.bfloat16)
    outgoing = (
        jnp.einsum("ts,tf->sf", dispatch, normed, preferred_element_type=jnp.float32)
        .astype(jnp.bfloat16)
        .reshape(expert_count, capacity, model_width)
    )
    slot_rows = lax.all_to_all(outgoing, EXP, split_axis=0, concat_axis=0, tiled=True)
    senders, slot_count, features = slot_rows.shape
    flat_rows = slot_rows.reshape(senders * slot_count, features)
    produced = expert_ffn(flat_rows, gate_experts, up_experts, down_experts)
    computed = produced.reshape(senders, slot_count, features)
    returned = lax.all_to_all(computed, EXP, split_axis=0, concat_axis=0, tiled=True)
    slot_gates = jnp.sum(jnp.where(hit, route_gates[:, :, None], 0.0), axis=1)
    combined = jnp.dot(
        slot_gates,
        returned.reshape(expert_count * capacity, model_width).astype(jnp.float32),
        precision=lax.Precision.HIGHEST,
        preferred_element_type=jnp.float32,
    )
    return (stream + combined).astype(jnp.bfloat16)


def solution(mesh):
    placed = (
        P(("req", "chip", "core"), None),
        P(("req", "chip", "core"), None),
        P(None, ("req", "chip", "core"), None),
        P(None, ("req", "chip", "core"), None),
        P(("req", "chip", "core"), None),
        P("req", None),
        P(),
        P(("req", "chip", "core"), None),
        P(("req", "chip", "core"), None),
        P(EXP, None, None),
        P(EXP, None, None),
        P(EXP, None, None),
    )
    req_count, exp_count = mesh.devices.shape
    split_mesh = Mesh(
        mesh.devices.reshape(req_count, exp_count // 2, 2), ("req", "chip", "core")
    )
    return jax.shard_map(
        on_device, mesh=split_mesh, in_specs=placed, out_specs=P(("req", "chip", "core"), None), check_vma=False
    )
```

```python
import math

import jax
import jax.numpy as jnp
from jax import lax
from jax.sharding import Mesh, PartitionSpec as P
from jax.experimental import pallas as pl
from jax.experimental.pallas import tpu as pltpu

QUERY_HEADS = 12
KEY_VALUE_HEADS = 2
HEAD_SIZE = 128


EPSILON = 1e-06
MASKED_SCORE = -1e30
EXP = ("chip", "core")


def head_scores(q_ref, keys, head):
    columns = slice(head * HEAD_SIZE, (head + 1) * HEAD_SIZE)
    contract = (((1,), (1,)), ((), ()))
    return lax.dot_general(
        q_ref[:, columns], keys, contract, preferred_element_type=jnp.float32
    ) * (1.0 / math.sqrt(HEAD_SIZE))


def local_kernel(rid_col_ref, rid_row_ref, q_ref, pkv_ref, skv_ref, acc_ref, peak_ref, total_ref):
    local_count = q_ref.shape[0]
    position = lax.broadcasted_iota(jnp.int32, (local_count, local_count), 0)
    key_position = lax.broadcasted_iota(jnp.int32, (local_count, local_count), 1)
    allowed = (rid_col_ref[...] == rid_row_ref[...]) & (position >= key_position)
    groups = QUERY_HEADS // KEY_VALUE_HEADS
    for head in range(QUERY_HEADS):
        kv_columns = slice((head // groups) * HEAD_SIZE, (head // groups + 1) * HEAD_SIZE)
        columns = slice(head * HEAD_SIZE, (head + 1) * HEAD_SIZE)
        prefix_scores = head_scores(q_ref, pkv_ref[0, :, kv_columns], head)
        suffix_scores = head_scores(q_ref, skv_ref[0, :, kv_columns], head)
        suffix_scores = jnp.where(allowed, suffix_scores, MASKED_SCORE)
        peak = jnp.maximum(
            jnp.max(prefix_scores, axis=1, keepdims=True),
            jnp.max(suffix_scores, axis=1, keepdims=True),
        )
        prefix_weights = jnp.exp(prefix_scores - peak)
        suffix_weights = jnp.where(allowed, jnp.exp(suffix_scores - peak), 0.0)
        total_ref[:, head : head + 1] = jnp.sum(prefix_weights, axis=1, keepdims=True) + jnp.sum(
            suffix_weights, axis=1, keepdims=True
        )
        peak_ref[:, head : head + 1] = peak
        acc_ref[:, columns] = jnp.dot(
            prefix_weights.astype(jnp.bfloat16),
            pkv_ref[1, :, kv_columns],
            preferred_element_type=jnp.float32,
        ) + jnp.dot(
            suffix_weights.astype(jnp.bfloat16),
            skv_ref[1, :, kv_columns],
            preferred_element_type=jnp.float32,
        )


def merge_kernel(q_ref, pkv_ref, acc_ref, peak_ref, total_ref, out_ref):
    groups = QUERY_HEADS // KEY_VALUE_HEADS
    for head in range(QUERY_HEADS):
        kv_columns = slice((head // groups) * HEAD_SIZE, (head // groups + 1) * HEAD_SIZE)
        columns = slice(head * HEAD_SIZE, (head + 1) * HEAD_SIZE)
        scores = head_scores(q_ref, pkv_ref[0, :, kv_columns], head)
        own_peak = jnp.max(scores, axis=1, keepdims=True)
        weights = jnp.exp(scores - own_peak)
        own_total = jnp.sum(weights, axis=1, keepdims=True)
        own_acc = jnp.dot(
            weights.astype(jnp.bfloat16), pkv_ref[1, :, kv_columns], preferred_element_type=jnp.float32
        )
        first_peak = peak_ref[:, head : head + 1]
        peak = jnp.maximum(first_peak, own_peak)
        first_scale = jnp.exp(first_peak - peak)
        own_scale = jnp.exp(own_peak - peak)
        total = total_ref[:, head : head + 1] * first_scale + own_total * own_scale
        summed = acc_ref[:, columns] * first_scale + own_acc * own_scale
        out_ref[:, columns] = (summed * (1.0 / total)).astype(out_ref.dtype)


def whole(shape):
    return pl.BlockSpec(shape, lambda: (0,) * len(shape))


def attend_local(queries, prefix_key_values, suffix_key_values, request_ids):
    local_count, model_width = queries.shape
    column, row = request_ids.reshape(local_count, 1), request_ids.reshape(1, local_count)
    inputs = (column, row, queries, prefix_key_values, suffix_key_values)
    stats = jax.ShapeDtypeStruct((local_count, QUERY_HEADS), jnp.float32)
    return pl.pallas_call(
        local_kernel,
        in_specs=[whole(x.shape) for x in inputs],
        out_specs=[whole((local_count, model_width)), whole(stats.shape), whole(stats.shape)],
        out_shape=[jax.ShapeDtypeStruct((local_count, model_width), jnp.float32), stats, stats],
        compiler_params=pltpu.CompilerParams(vmem_limit_bytes=48 * 1024 * 1024),
    )(*inputs)


def attend_merge(queries, prefix_key_values, acc, peak, total):
    inputs = (queries, prefix_key_values, acc, peak, total)
    return pl.pallas_call(
        merge_kernel,
        in_specs=[whole(x.shape) for x in inputs],
        out_specs=whole(queries.shape),
        out_shape=jax.ShapeDtypeStruct(queries.shape, jnp.bfloat16),
        compiler_params=pltpu.CompilerParams(vmem_limit_bytes=48 * 1024 * 1024),
    )(*inputs)


def expert_kernel(rows_ref, gate_ref, up_ref, down_ref, out_ref, acc_ref):
    step = pl.program_id(0)
    first = step == 0
    last = step == pl.num_programs(0) - 1
    rows = rows_ref[...]
    gated = jnp.dot(rows, gate_ref[...], preferred_element_type=jnp.float32)
    lifted = jnp.dot(rows, up_ref[...], preferred_element_type=jnp.float32)
    active = (jnp.maximum(gated, 0.0) * lifted).astype(jnp.bfloat16)
    part = jnp.dot(active, down_ref[...], preferred_element_type=jnp.float32)

    @pl.when(first & jnp.logical_not(last))
    def _():
        acc_ref[...] = part

    @pl.when(jnp.logical_not(first) & jnp.logical_not(last))
    def _():
        acc_ref[...] += part

    @pl.when(last & jnp.logical_not(first))
    def _():
        out_ref[...] = (acc_ref[...] + part).astype(out_ref.dtype)

    @pl.when(first & last)
    def _():
        out_ref[...] = part.astype(out_ref.dtype)


def expert_ffn(rows, gate_experts, up_experts, down_experts):
    count, width = rows.shape
    hidden = gate_experts.shape[2]
    block = 256 if hidden % 256 == 0 else hidden
    return pl.pallas_call(
        expert_kernel,
        grid=(hidden // block,),
        in_specs=[
            pl.BlockSpec((count, width), lambda f: (0, 0)),
            pl.BlockSpec((None, width, block), lambda f: (0, 0, f)),
            pl.BlockSpec((None, width, block), lambda f: (0, 0, f)),
            pl.BlockSpec((None, block, width), lambda f: (0, f, 0)),
        ],
        out_specs=pl.BlockSpec((count, width), lambda f: (0, 0)),
        out_shape=jax.ShapeDtypeStruct((count, width), jnp.bfloat16),
        scratch_shapes=[pltpu.VMEM((count, width), jnp.float32)],
        compiler_params=pltpu.CompilerParams(vmem_limit_bytes=48 * 1024 * 1024),
    )(rows, gate_experts, up_experts, down_experts)


def on_device(
    residual,
    queries,
    suffix_key_values,
    prefix_key_values,
    request_ids,
    out_weight,
    norm_gain,
    expert_routes,
    route_gates,
    gate_experts,
    up_experts,
    down_experts,
):
    local_count = queries.shape[0]
    model_width = queries.shape[1]
    chip_count = lax.axis_size("chip")
    req_count = lax.axis_size("req")
    by_req = lax.all_to_all(
        jnp.broadcast_to(prefix_key_values[:, None], (2, req_count) + prefix_key_values.shape[1:]),
        "req",
        split_axis=1,
        concat_axis=1,
        tiled=True,
    ).reshape(2, req_count * prefix_key_values.shape[1], prefix_key_values.shape[2])
    spread = jnp.broadcast_to(by_req[:, None], (2, chip_count) + by_req.shape[1:])
    by_chip = lax.all_to_all(spread, "chip", split_axis=1, concat_axis=1, tiled=True).reshape(
        2, chip_count * by_req.shape[1], by_req.shape[2]
    )
    partner_half = lax.ppermute(by_chip, "core", [(0, 1), (1, 0)])
    acc, peak, total = attend_local(queries, by_chip, suffix_key_values, request_ids)
    attended = attend_merge(queries, partner_half, acc, peak, total)
    section = attended
    projected = jnp.dot(
        section,
        lax.all_gather(out_weight, "req", axis=0, tiled=True),
        preferred_element_type=jnp.float32,
    )
    stream = residual.astype(jnp.float32) + projected
    inverse_rms = lax.rsqrt(jnp.mean(stream * stream, axis=1, keepdims=True) + EPSILON)
    normed = (stream * inverse_rms * norm_gain[None, :]).astype(jnp.bfloat16)
    top_count = expert_routes.shape[1]
    expert_count = gate_experts.shape[0] * lax.axis_size(EXP)
    capacity = 3 * top_count * local_count // (2 * expert_count)
    flat_routes = expert_routes.reshape(-1)
    matches = (flat_routes[:, None] == jnp.arange(expert_count, dtype=jnp.int32)[None, :]).astype(
        jnp.int32
    )
    route_count = flat_routes.shape[0]
    earlier = (
        lax.broadcasted_iota(jnp.int32, (route_count, route_count), 0)
        > lax.broadcasted_iota(jnp.int32, (route_count, route_count), 1)
    ).astype(jnp.bfloat16)
    before = jnp.dot(earlier, matches.astype(jnp.bfloat16), preferred_element_type=jnp.float32)
    slot_rank = jnp.sum(before.astype(jnp.int32) * matches, axis=1)
    slot_of_route = flat_routes * capacity + slot_rank
    slot_ids = jnp.arange(expert_count * capacity, dtype=jnp.int32)
    hit = slot_of_route.reshape(local_count, top_count)[:, :, None] == slot_ids[None, None, :]
    dispatch = jnp.any(hit, axis=1).astype(jnp.bfloat16)
    outgoing = (
        jnp.einsum("ts,tf->sf", dispatch, normed, preferred_element_type=jnp.float32)
        .astype(jnp.bfloat16)
        .reshape(expert_count, capacity, model_width)
    )
    slot_rows = lax.all_to_all(outgoing, EXP, split_axis=0, concat_axis=0, tiled=True)
    senders, slot_count, features = slot_rows.shape
    flat_rows = slot_rows.reshape(senders * slot_count, features)
    produced = expert_ffn(flat_rows, gate_experts, up_experts, down_experts)
    computed = produced.reshape(senders, slot_count, features)
    returned = lax.all_to_all(computed, EXP, split_axis=0, concat_axis=0, tiled=True)
    slot_gates = jnp.sum(jnp.where(hit, route_gates[:, :, None], 0.0), axis=1)
    combined = jnp.dot(
        slot_gates,
        returned.reshape(expert_count * capacity, model_width).astype(jnp.float32),
        precision=lax.Precision.HIGHEST,
        preferred_element_type=jnp.float32,
    )
    return (stream + combined).astype(jnp.bfloat16)


def solution(mesh):
    placed = (
        P(("req", "chip", "core"), None),
        P(("req", "chip", "core"), None),
        P(None, ("req", "chip", "core"), None),
        P(None, ("req", "chip", "core"), None),
        P(("req", "chip", "core"), None),
        P("req", None),
        P(),
        P(("req", "chip", "core"), None),
        P(("req", "chip", "core"), None),
        P(EXP, None, None),
        P(EXP, None, None),
        P(EXP, None, None),
    )
    req_count, exp_count = mesh.devices.shape
    split_mesh = Mesh(
        mesh.devices.reshape(req_count, exp_count // 2, 2), ("req", "chip", "core")
    )
    return jax.shard_map(
        on_device, mesh=split_mesh, in_specs=placed, out_specs=P(("req", "chip", "core"), None), check_vma=False
    )
```
